256 devices in a mesh: wide: 64 (over y, z, core), seq: 4 (over x).
Axes of the slice: x: 4, y: 4, z: 8, core: 2. Of those that a mesh axis runs over, the one named last changes fastest.
Arguments:
- power: bfloat16 [160, 2097152], P('seq', 'wide')
- bin_index: int32 [160], P('seq'), may hold values from 0 to 7, as said below
- session: int32 [16384], replicated, may hold values from 0 to 63, as said below
- readin_weight: bfloat16 [64, 128, 2048], P('wide'), may hold values from -0.5 to 0.5
- qkv_weight: bfloat16 [2048, 1536], replicated, may hold values from -0.125 to 0.125
Outputs:
- heads: bfloat16 [16384, 8, 1024], P(('wide', 'seq'))
The draws below stay inside these ranges and needn't reach their ends.
Inputs may be any that keep to these rules, and one draw needn't show every extreme that they name: `bin_index`: the samples j * 40 to (j + 1) * 40 - 1 name only bins j * 2 to (j + 1) * 2 - 1. In each aligned block of 64 patches (patches k * 64 to (k + 1) * 64 - 1) no session is named by more than 2 patches; one session, the same for every block, is named by exactly 2 patches of every block.
All inputs are finite; a program needn't handle non-finite values.
Results may differ from the reference program's by a relative error of at most 0.008.
Values may be sent and summed in bfloat16 or wider, within the bound.
No kernel may reach another device: no remote copies, remote signals or barrier semaphores. Data moves between devices by JAX's collectives and lax.ppermute only.
A program may use at most 64 MiB of HBM per device.

```python
import math
import jax
import jax.numpy as jnp
from jax import lax

CH = 128
D = 2048
HD = 128
HEADS = 8
KVH = 2
SPB = 20
QP = 64
BIN_DEV = 2
QKV = 1536
PATCH_DEV = 256
SAMP_DEV = 40
BINS = 8
SAMPLES = 160
PATCHES = 16384
CHANNELS = 2097152
SESSIONS = 64
CAP = 2
N_WIDE = 64


def draw_power(key, part):
    key_noise, key_rows, key_cols = jax.random.split(key, 3)
    moment = jnp.arange(SAMPLES, dtype=jnp.float32)
    rising = 1.0 + 2.0 * moment / max(SAMPLES - 1, 1)
    noise_part = jnp.exp(0.5 * jax.random.normal(key_noise, (SAMPLES, CHANNELS), jnp.float32))
    row_scale = jnp.exp(jax.random.uniform(key_rows, (SAMPLES,), jnp.float32, 0.0, math.log(10.0)))
    col_scale = jnp.exp(jax.random.uniform(key_cols, (CHANNELS,), jnp.float32, 0.0, math.log(10.0)))
    return (noise_part * (row_scale * rising)[:, None] * col_scale[None, :]).astype(jnp.bfloat16)


def draw_bin_index(key, part):
    moment = jnp.arange(SAMPLES, dtype=jnp.int32)
    shard_number = moment // SAMP_DEV
    inside = moment % SAMP_DEV
    jitter = jax.random.randint(key, (SAMPLES,), -4, 5)
    local_bin = jnp.clip((inside + jitter) // SPB, 0, BIN_DEV - 1)
    return (shard_number * BIN_DEV + local_bin).astype(jnp.int32)


def draw_session(key, part):
    key_hot, key_blocks = jax.random.split(key)
    block_total = PATCHES // QP
    hot_session = jax.random.randint(key_hot, (), 0, SESSIONS)
    others = jnp.arange((SESSIONS - 1) * CAP, dtype=jnp.int32) // CAP
    others = others + (others >= hot_session).astype(jnp.int32)

    def one_block(block_key):
        first_key, second_key = jax.random.split(block_key)
        picked = jax.random.permutation(first_key, others)[:QP - CAP]
        filled = jnp.concatenate([jnp.full((CAP,), hot_session, jnp.int32), picked])
        return jax.random.permutation(second_key, filled)
    blocks = jax.vmap(one_block)(jax.random.split(key_blocks, block_total))
    return blocks.reshape(PATCHES).astype(jnp.int32)


def level_of(own_key, dims, shards, least, high):
    level, own = 1.0, jax.random.fold_in(own_key, 6)
    for axis_at, blocks in shards:
        heights = jnp.exp(jax.random.uniform(jax.random.fold_in(own, axis_at), (blocks,), jnp.float32, least / len(shards), high / len(shards)))
        level = level * jnp.repeat(heights, dims[axis_at] // blocks).reshape([-1 if axis == axis_at else 1 for axis in range(len(dims))])
    return level


def noise(own_key, shape, deviation, most, pieces=(), kind=jnp.bfloat16):
    factor_of = level_of(own_key, shape, pieces, -0.22, 0.18) if pieces else 1.0
    drawn = jax.random.normal(own_key, shape, jnp.float32) * deviation * factor_of
    return jnp.minimum(jnp.maximum(drawn, -most), most).astype(kind)


def setup_inputs(seed: int = 0) -> dict:
    streams_of = jax.random.split(jax.random.key(seed), 6)
    power = draw_power(jax.random.fold_in(streams_of[5], 71), 0)
    bin_index = draw_bin_index(jax.random.fold_in(streams_of[5], 71), 0)
    session = draw_session(jax.random.fold_in(streams_of[5], 71), 0)
    readin_weight = noise(streams_of[3], (SESSIONS, CH, D), CH ** -0.5, 0.5, ((0, 64),))
    qkv_weight = noise(streams_of[4], (D, QKV), D ** -0.5, 0.125)
    return {"power": power, "bin_index": bin_index, "session": session, "readin_weight": readin_weight, "qkv_weight": qkv_weight}


def attention_heads(qkv_rows):
    row_count = qkv_rows.shape[0]
    length = qkv_rows.shape[1]
    group_size = HEADS // KVH
    values = qkv_rows.astype(jnp.float32)
    queries = values[:, :, :HEADS * HD].reshape(row_count, length, KVH, group_size, HD)
    key_rows = values[:, :, HEADS * HD:(HEADS + KVH) * HD].reshape(row_count, length, KVH, HD)
    value_rows = values[:, :, (HEADS + KVH) * HD:].reshape(row_count, length, KVH, HD)
    queries = queries / jnp.sqrt(lax.optimization_barrier(jnp.mean(queries * queries, axis=-1, keepdims=True)) + 1e-06)
    key_rows = key_rows / jnp.sqrt(lax.optimization_barrier(jnp.mean(key_rows * key_rows, axis=-1, keepdims=True)) + 1e-06)
    scores = jnp.einsum('pigrd,pjgd->pgrij', queries, key_rows) / HD ** 0.5
    exponent = jnp.exp(scores)
    weights = (exponent / lax.optimization_barrier(jnp.sum(exponent, axis=-1, keepdims=True))).astype(jnp.bfloat16)
    mixed = jnp.einsum('pgrij,pjgd->pigrd', weights.astype(jnp.float32), value_rows)
    return mixed.reshape(row_count, length, HEADS * HD).astype(jnp.bfloat16)

def reference(power, bin_index, session, readin_weight, qkv_weight):
    onehot = (bin_index[:, None] == jnp.arange(BINS, dtype=jnp.int32)[None, :]).astype(jnp.float32)
    block_width = PATCH_DEV * CH

    def one_column(column):
        power_block = lax.dynamic_slice_in_dim(power, column * block_width, block_width, 1).astype(jnp.float32)
        inv_rms = 1.0 / jnp.sqrt(lax.optimization_barrier(jnp.sum(power_block * power_block, axis=0)) / SAMPLES + 1e-06)
        active = jnp.maximum(power_block * inv_rms[None, :] - 0.8, 0.0)
        binned = (jnp.dot(onehot.T, active, precision=lax.Precision.HIGHEST) * (1.0 / SPB)).astype(jnp.bfloat16)
        patches = binned.reshape(BINS, PATCH_DEV, CH).transpose(1, 0, 2)
        owners = lax.dynamic_slice_in_dim(session, column * PATCH_DEV, PATCH_DEV).astype(jnp.int32)
        chosen = readin_weight[owners]
        tokens = jnp.einsum('pbc,pcd->pbd', patches.astype(jnp.float32), chosen.astype(jnp.float32)).astype(jnp.bfloat16)
        product = jnp.dot(tokens.reshape(PATCH_DEV * BINS, D), qkv_weight, preferred_element_type=jnp.float32)
        qkv_rows = product.astype(jnp.bfloat16).reshape(PATCH_DEV, BINS, QKV)
        return attention_heads(qkv_rows)
    columns = lax.map(one_column, jnp.arange(N_WIDE, dtype=jnp.int32))
    return columns.reshape(PATCHES, BINS, HEADS * HD)
```

```python
import jax
import jax.numpy as jnp
from jax import lax
from jax.sharding import PartitionSpec as P

CH = 128
HD = 128
HEADS = 8
KVH = 2
SPB = 20
CAP = 2


def attention_heads(qkv_rows):
    row_count = qkv_rows.shape[0]
    length = qkv_rows.shape[1]
    group_size = HEADS // KVH
    values = qkv_rows.astype(jnp.float32)
    queries = values[:, :, : HEADS * HD].reshape(row_count, length, KVH, group_size, HD)
    key_rows = values[:, :, HEADS * HD : (HEADS + KVH) * HD].reshape(row_count, length, KVH, HD)
    value_rows = values[:, :, (HEADS + KVH) * HD :].reshape(row_count, length, KVH, HD)
    queries = queries / jnp.sqrt(jnp.mean(queries * queries, axis=-1, keepdims=True) + 1e-06)
    key_rows = key_rows / jnp.sqrt(jnp.mean(key_rows * key_rows, axis=-1, keepdims=True) + 1e-06)
    scores = jnp.einsum("pigrd,pjgd->pgrij", queries, key_rows) / HD**0.5
    exponent = jnp.exp(scores)
    weights = (exponent / jnp.sum(exponent, axis=-1, keepdims=True)).astype(jnp.bfloat16)
    mixed = jnp.einsum("pgrij,pjgd->pigrd", weights.astype(jnp.float32), value_rows)
    return mixed.reshape(row_count, length, HEADS * HD).astype(jnp.bfloat16)


def body(power, bin_index, session, readin_weight, qkv_weight):
    wide_count = lax.axis_size("wide")
    seq_count = lax.axis_size("seq")
    wide_index = lax.axis_index("wide")
    seq_index = lax.axis_index("seq")
    sample_rows, channels = power.shape
    patch_count = channels // CH
    quarter = patch_count // seq_count
    bin_count = sample_rows // SPB
    all_bins = bin_count * seq_count

    signal = power.astype(jnp.float32)
    partial = jnp.sum(signal * signal, axis=0)
    spread = jnp.broadcast_to(partial[None, :], (seq_count, channels))
    gathered = lax.all_to_all(spread, "seq", split_axis=0, concat_axis=0, tiled=True)
    squares = jnp.sum(gathered, axis=0)
    inv_rms = 1.0 / jnp.sqrt(squares / (sample_rows * seq_count) + 1e-06)
    active = jnp.maximum(signal * inv_rms[None, :] - 0.8, 0.0)
    local_bins = bin_index - seq_index * bin_count
    onehot = (local_bins[:, None] == jnp.arange(bin_count, dtype=jnp.int32)[None, :]).astype(
        jnp.float32
    )
    binned = (jnp.dot(onehot.T, active, precision=lax.Precision.HIGHEST) * (1.0 / SPB)).astype(
        jnp.bfloat16
    )
    binned = binned.reshape(bin_count, seq_count, quarter, CH).transpose(1, 0, 2, 3)
    binned = lax.all_to_all(binned, "seq", split_axis=0, concat_axis=0, tiled=True)
    block_rows = binned.reshape(all_bins, quarter, CH).transpose(1, 0, 2).reshape(
        quarter, all_bins * CH
    )

    block = wide_index * seq_count + seq_index
    owners = lax.dynamic_slice_in_dim(session, block * quarter, quarter)
    same = owners[:, None] == owners[None, :]
    earlier = jnp.arange(quarter)[None, :] < jnp.arange(quarter)[:, None]
    rank = jnp.sum((same & earlier).astype(jnp.int32), axis=1)
    slot = owners * CAP + rank
    slot_count = wide_count * CAP
    dispatch = (jnp.arange(slot_count, dtype=jnp.int32)[:, None] == slot[None, :]).astype(
        jnp.bfloat16
    )
    outgoing = jnp.dot(dispatch, block_rows, preferred_element_type=jnp.float32).astype(
        jnp.bfloat16
    )
    arrived = lax.all_to_all(outgoing, "wide", split_axis=0, concat_axis=0, tiled=True)
    weight_block = readin_weight[0]
    tokens = jnp.dot(
        arrived.reshape(slot_count * all_bins, CH), weight_block, preferred_element_type=jnp.float32
    ).astype(jnp.bfloat16)
    tokens = tokens.reshape(slot_count, all_bins * weight_block.shape[1])
    returned = lax.all_to_all(tokens, "wide", split_axis=0, concat_axis=0, tiled=True)
    mine = jnp.dot(dispatch.T, returned, preferred_element_type=jnp.float32).astype(jnp.bfloat16)
    mine = mine.reshape(quarter * all_bins, weight_block.shape[1])
    projected = jnp.dot(mine, qkv_weight, preferred_element_type=jnp.float32).astype(jnp.bfloat16)
    projected = projected.reshape(quarter, all_bins, qkv_weight.shape[1])
    return attention_heads(projected)


def solution(mesh):
    placed = (P("seq", "wide"), P("seq"), P(), P("wide", None, None), P())
    return jax.shard_map(
        body, mesh=mesh, in_specs=placed, out_specs=P(("wide", "seq"), None, None), check_vma=False
    )
```

```python
import jax
import jax.numpy as jnp
from jax import lax
from jax.sharding import PartitionSpec as P

CH = 128
HD = 128
HEADS = 8
KVH = 2
SPB = 20
CAP = 2


def attention_heads(qkv_rows):
    row_count = qkv_rows.shape[0]
    length = qkv_rows.shape[1]
    group_size = HEADS // KVH
    values = qkv_rows.astype(jnp.float32)
    queries = values[:, :, : HEADS * HD].reshape(row_count, length, KVH, group_size, HD)
    key_rows = values[:, :, HEADS * HD : (HEADS + KVH) * HD].reshape(row_count, length, KVH, HD)
    value_rows = values[:, :, (HEADS + KVH) * HD :].reshape(row_count, length, KVH, HD)
    queries = queries / jnp.sqrt(jnp.mean(queries * queries, axis=-1, keepdims=True) + 1e-06)
    key_rows = key_rows / jnp.sqrt(jnp.mean(key_rows * key_rows, axis=-1, keepdims=True) + 1e-06)
    scores = jnp.einsum("pigrd,pjgd->pgrij", queries, key_rows) / HD**0.5
    exponent = jnp.exp(scores)
    weights = (exponent / jnp.sum(exponent, axis=-1, keepdims=True)).astype(jnp.bfloat16)
    mixed = jnp.einsum("pgrij,pjgd->pigrd", weights.astype(jnp.float32), value_rows)
    return mixed.reshape(row_count, length, HEADS * HD).astype(jnp.bfloat16)


def body(power, bin_index, session, readin_weight, qkv_weight):
    wide_count = lax.axis_size("wide")
    seq_count = lax.axis_size("seq")
    wide_index = lax.axis_index("wide")
    seq_index = lax.axis_index("seq")
    sample_rows, channels = power.shape
    patch_count = channels // CH
    quarter = patch_count // seq_count
    bin_count = sample_rows // SPB
    all_bins = bin_count * seq_count

    signal = power.astype(jnp.float32)
    partial = jnp.sum(signal * signal, axis=0)
    spread = jnp.broadcast_to(partial[None, :], (seq_count, channels))
    gathered = lax.all_to_all(spread, "seq", split_axis=0, concat_axis=0, tiled=True)
    squares = jnp.sum(gathered, axis=0)
    inv_rms = 1.0 / jnp.sqrt(squares / (sample_rows * seq_count) + 1e-06)
    active = jnp.maximum(signal * inv_rms[None, :] - 0.8, 0.0)
    local_bins = bin_index - seq_index * bin_count
    onehot = (local_bins[:, None] == jnp.arange(bin_count, dtype=jnp.int32)[None, :]).astype(
        jnp.float32
    )
    binned = (jnp.dot(onehot.T, active, precision=lax.Precision.HIGHEST) * (1.0 / SPB)).astype(
        jnp.bfloat16
    )
    binned = binned.reshape(bin_count, seq_count, quarter, CH).transpose(1, 0, 2, 3)
    binned = lax.all_to_all(binned, "seq", split_axis=0, concat_axis=0, tiled=True)
    block_rows = binned.reshape(all_bins, quarter, CH).transpose(1, 0, 2).reshape(
        quarter, all_bins * CH
    )

    block = wide_index * seq_count + seq_index
    owners = lax.dynamic_slice_in_dim(session, block * quarter, quarter)
    same = owners[:, None] == owners[None, :]
    earlier = jnp.arange(quarter)[None, :] < jnp.arange(quarter)[:, None]
    rank = jnp.sum((same & earlier).astype(jnp.int32), axis=1)
    slot = owners * CAP + rank
    slot_count = wide_count * CAP
    dispatch = (jnp.arange(slot_count, dtype=jnp.int32)[:, None] == slot[None, :]).astype(
        jnp.bfloat16
    )
    outgoing = jnp.dot(dispatch, block_rows, preferred_element_type=jnp.float32).astype(
        jnp.bfloat16
    )
    arrived = lax.all_to_all(outgoing, "wide", split_axis=0, concat_axis=0, tiled=True)
    weight_block = readin_weight[0]
    tokens = jnp.dot(
        arrived.reshape(slot_count * all_bins, CH), weight_block, preferred_element_type=jnp.float32
    ).astype(jnp.bfloat16)
    projected = jnp.dot(tokens, qkv_weight, preferred_element_type=jnp.float32).astype(jnp.bfloat16)
    projected = projected.reshape(slot_count, all_bins, qkv_weight.shape[1])
    heads = attention_heads(projected)
    width = heads.shape[2]
    returned = lax.all_to_all(
        heads.reshape(slot_count, all_bins * width), "wide", split_axis=0, concat_axis=0, tiled=True
    )
    mine = jnp.dot(dispatch.T, returned, preferred_element_type=jnp.float32).astype(jnp.bfloat16)
    return mine.reshape(quarter, all_bins, width)


def solution(mesh):
    placed = (P("seq", "wide"), P("seq"), P(), P("wide", None, None), P())
    return jax.shard_map(
        body, mesh=mesh, in_specs=placed, out_specs=P(("wide", "seq"), None, None), check_vma=False
    )
```

```python
import jax
import jax.numpy as jnp
from jax import lax
from jax.experimental import pallas as pl
from jax.sharding import PartitionSpec as P

CH = 128
HD = 128
HEADS = 8
KVH = 2
SPB = 20
CAP = 2
ROWS = 128


def _attention_kernel(x_ref, o_ref):
    rows = x_ref.shape[0]
    length = 8
    row_patch = lax.broadcasted_iota(jnp.int32, (rows, rows), 0) // length
    col_patch = lax.broadcasted_iota(jnp.int32, (rows, rows), 1) // length
    same = row_patch == col_patch
    group_size = HEADS // KVH
    for g in range(KVH):
        k = x_ref[:, (HEADS + g) * HD : (HEADS + g + 1) * HD].astype(jnp.float32)
        k = k / jnp.sqrt(jnp.mean(k * k, axis=-1, keepdims=True) + 1e-06)
        v = x_ref[:, (HEADS + KVH + g) * HD : (HEADS + KVH + g + 1) * HD]
        for r in range(group_size):
            h = g * group_size + r
            q = x_ref[:, h * HD : (h + 1) * HD].astype(jnp.float32)
            q = q / jnp.sqrt(jnp.mean(q * q, axis=-1, keepdims=True) + 1e-06)
            s = lax.dot_general(
                q, k, (((1,), (1,)), ((), ())), precision=lax.Precision.HIGHEST,
                preferred_element_type=jnp.float32,
            ) / HD**0.5
            e = jnp.where(same, jnp.exp(s), 0.0)
            w = (e / jnp.sum(e, axis=-1, keepdims=True)).astype(jnp.bfloat16)
            o = jnp.dot(w, v, preferred_element_type=jnp.float32)
            o_ref[:, h * HD : (h + 1) * HD] = o.astype(jnp.bfloat16)


def attention_kernel(qkv_rows):
    count, length, width = qkv_rows.shape
    flat = qkv_rows.reshape(count * length, width)
    total = count * length
    out = pl.pallas_call(
        _attention_kernel,
        out_shape=jax.ShapeDtypeStruct((total, HEADS * HD), jnp.bfloat16),
        grid=(total // ROWS,),
        in_specs=[pl.BlockSpec((ROWS, width), lambda i: (i, 0))],
        out_specs=pl.BlockSpec((ROWS, HEADS * HD), lambda i: (i, 0)),
    )(flat)
    return out.reshape(count, length, HEADS * HD)


def attention_heads(qkv_rows):
    row_count = qkv_rows.shape[0]
    length = qkv_rows.shape[1]
    group_size = HEADS // KVH
    values = qkv_rows.astype(jnp.float32)
    queries = values[:, :, : HEADS * HD].reshape(row_count, length, KVH, group_size, HD)
    key_rows = values[:, :, HEADS * HD : (HEADS + KVH) * HD].reshape(row_count, length, KVH, HD)
    value_rows = values[:, :, (HEADS + KVH) * HD :].reshape(row_count, length, KVH, HD)
    queries = queries / jnp.sqrt(jnp.mean(queries * queries, axis=-1, keepdims=True) + 1e-06)
    key_rows = key_rows / jnp.sqrt(jnp.mean(key_rows * key_rows, axis=-1, keepdims=True) + 1e-06)
    scores = jnp.einsum("pigrd,pjgd->pgrij", queries, key_rows) / HD**0.5
    exponent = jnp.exp(scores)
    weights = (exponent / jnp.sum(exponent, axis=-1, keepdims=True)).astype(jnp.bfloat16)
    mixed = jnp.einsum("pgrij,pjgd->pigrd", weights.astype(jnp.float32), value_rows)
    return mixed.reshape(row_count, length, HEADS * HD).astype(jnp.bfloat16)


def body(power, bin_index, session, readin_weight, qkv_weight):
    wide_count = lax.axis_size("wide")
    seq_count = lax.axis_size("seq")
    wide_index = lax.axis_index("wide")
    seq_index = lax.axis_index("seq")
    sample_rows, channels = power.shape
    patch_count = channels // CH
    quarter = patch_count // seq_count
    bin_count = sample_rows // SPB
    all_bins = bin_count * seq_count

    signal = power.astype(jnp.float32)
    partial = jnp.sum(signal * signal, axis=0)
    spread = jnp.broadcast_to(partial[None, :], (seq_count, channels))
    gathered = lax.all_to_all(spread, "seq", split_axis=0, concat_axis=0, tiled=True)
    squares = jnp.sum(gathered, axis=0)
    inv_rms = 1.0 / jnp.sqrt(squares / (sample_rows * seq_count) + 1e-06)
    active = jnp.maximum(signal * inv_rms[None, :] - 0.8, 0.0)
    local_bins = bin_index - seq_index * bin_count
    onehot = (local_bins[:, None] == jnp.arange(bin_count, dtype=jnp.int32)[None, :]).astype(
        jnp.float32
    )
    binned = (jnp.dot(onehot.T, active, precision=lax.Precision.HIGHEST) * (1.0 / SPB)).astype(
        jnp.bfloat16
    )
    binned = binned.reshape(bin_count, seq_count, quarter, CH).transpose(1, 0, 2, 3)
    binned = lax.all_to_all(binned, "seq", split_axis=0, concat_axis=0, tiled=True)
    block_rows = binned.reshape(all_bins, quarter, CH).transpose(1, 0, 2).reshape(
        quarter, all_bins * CH
    )

    block = wide_index * seq_count + seq_index
    owners = lax.dynamic_slice_in_dim(session, block * quarter, quarter)
    same = owners[:, None] == owners[None, :]
    earlier = jnp.arange(quarter)[None, :] < jnp.arange(quarter)[:, None]
    rank = jnp.sum((same & earlier).astype(jnp.int32), axis=1)
    slot = owners * CAP + rank
    slot_count = wide_count * CAP
    dispatch = (jnp.arange(slot_count, dtype=jnp.int32)[:, None] == slot[None, :]).astype(
        jnp.bfloat16
    )
    outgoing = jnp.dot(dispatch, block_rows, preferred_element_type=jnp.float32).astype(
        jnp.bfloat16
    )
    arrived = lax.all_to_all(outgoing, "wide", split_axis=0, concat_axis=0, tiled=True)
    weight_block = readin_weight[0]
    merged = jnp.dot(weight_block, qkv_weight, preferred_element_type=jnp.float32)
    merged_hi = merged.astype(jnp.bfloat16)
    merged_lo = (merged - merged_hi.astype(jnp.float32)).astype(jnp.bfloat16)
    rows = arrived.reshape(slot_count * all_bins, CH)
    projected = jnp.dot(rows, merged_hi, preferred_element_type=jnp.float32) + jnp.dot(
        rows, merged_lo, preferred_element_type=jnp.float32
    )
    projected = projected.astype(jnp.bfloat16).reshape(slot_count, all_bins, qkv_weight.shape[1])
    heads = attention_kernel(projected)
    width = heads.shape[2]
    returned = lax.all_to_all(
        heads.reshape(slot_count, all_bins * width), "wide", split_axis=0, concat_axis=0, tiled=True
    )
    mine = jnp.dot(dispatch.T, returned, preferred_element_type=jnp.float32).astype(jnp.bfloat16)
    return mine.reshape(quarter, all_bins, width)


def solution(mesh):
    placed = (P("seq", "wide"), P("seq"), P(), P("wide", None, None), P())
    return jax.shard_map(
        body, mesh=mesh, in_specs=placed, out_specs=P(("wide", "seq"), None, None), check_vma=False
    )
```

```python
import jax
import jax.numpy as jnp
from jax import lax
from jax.experimental import pallas as pl
from jax.sharding import PartitionSpec as P

CH = 128
HD = 128
HEADS = 8
KVH = 2
SPB = 20
CAP = 2
BINS = 8
ROWS = 128
SUB = 4


def _weights_kernel(x_ref, o_ref):
    group_size = HEADS // KVH
    sub_rows = SUB * BINS
    cols = SUB * group_size * BINS
    row_patch = lax.broadcasted_iota(jnp.int32, (sub_rows, cols), 0) // BINS
    col_patch = lax.broadcasted_iota(jnp.int32, (sub_rows, cols), 1) // (group_size * BINS)
    same = row_patch == col_patch
    for sg in range(x_ref.shape[0] // sub_rows):
        base = sg * sub_rows
        xs = x_ref[base : base + sub_rows, :].astype(jnp.float32)
        for g in range(KVH):
            k = xs[:, (HEADS + g) * HD : (HEADS + g + 1) * HD]
            k = k / jnp.sqrt(jnp.mean(k * k, axis=-1, keepdims=True) + 1e-06)
            pieces = []
            for p in range(SUB):
                for r in range(group_size):
                    h = g * group_size + r
                    pieces.append(xs[p * BINS : (p + 1) * BINS, h * HD : (h + 1) * HD])
            q = jnp.concatenate(pieces, axis=0)
            q = q / jnp.sqrt(jnp.mean(q * q, axis=-1, keepdims=True) + 1e-06)
            s = lax.dot_general(
                k, q, (((1,), (1,)), ((), ())), precision=lax.Precision.HIGHEST,
                preferred_element_type=jnp.float32,
            ) / HD**0.5
            e = jnp.where(same, jnp.exp(s), 0.0)
            w = (e / jnp.sum(e, axis=0, keepdims=True)).astype(jnp.bfloat16).astype(jnp.float32)
            width = group_size * BINS
            for p in range(SUB):
                tile = w[p * BINS : (p + 1) * BINS, :]
                compact = tile[:, 0:width]
                for c in range(1, SUB):
                    compact = compact + tile[:, c * width : (c + 1) * width]
                row0 = base + p * BINS
                o_ref[row0 : row0 + BINS, g * width : (g + 1) * width] = compact


def attention_weights(qkv_flat):
    total, width = qkv_flat.shape
    return pl.pallas_call(
        _weights_kernel,
        out_shape=jax.ShapeDtypeStruct((total, HEADS * BINS), jnp.float32),
        grid=(total // ROWS,),
        in_specs=[pl.BlockSpec((ROWS, width), lambda i: (i, 0))],
        out_specs=pl.BlockSpec((ROWS, HEADS * BINS), lambda i: (i, 0)),
    )(qkv_flat)


def heads_from(weights, values):
    n = weights.shape[0]
    group_size = HEADS // KVH
    w = weights.reshape(n, BINS, KVH, group_size, BINS)
    v = values.reshape(n, BINS, KVH, HD)
    mixed = jnp.einsum("pjgri,pjge->pigre", w, v, preferred_element_type=jnp.float32)
    return mixed.reshape(n, BINS, HEADS * HD).astype(jnp.bfloat16)


def body(power, bin_index, session, readin_weight, qkv_weight):
    wide_count = lax.axis_size("wide")
    seq_count = lax.axis_size("seq")
    wide_index = lax.axis_index("wide")
    seq_index = lax.axis_index("seq")
    sample_rows, channels = power.shape
    patch_count = channels // CH
    quarter = patch_count // seq_count
    bin_count = sample_rows // SPB
    all_bins = bin_count * seq_count

    signal = power.astype(jnp.float32)
    partial = jnp.sum(signal * signal, axis=0)
    spread = jnp.broadcast_to(partial[None, :], (seq_count, channels))
    gathered = lax.all_to_all(spread, "seq", split_axis=0, concat_axis=0, tiled=True)
    squares = jnp.sum(gathered, axis=0)
    inv_rms = 1.0 / jnp.sqrt(squares / (sample_rows * seq_count) + 1e-06)
    active = jnp.maximum(signal * inv_rms[None, :] - 0.8, 0.0)
    local_bins = bin_index - seq_index * bin_count
    onehot = (local_bins[:, None] == jnp.arange(bin_count, dtype=jnp.int32)[None, :]).astype(
        jnp.float32
    )
    binned = (jnp.dot(onehot.T, active, precision=lax.Precision.HIGHEST) * (1.0 / SPB)).astype(
        jnp.bfloat16
    )
    binned = binned.reshape(bin_count, seq_count, quarter, CH).transpose(1, 0, 2, 3)
    binned = lax.all_to_all(binned, "seq", split_axis=0, concat_axis=0, tiled=True)
    block_rows = binned.reshape(all_bins, quarter, CH).transpose(1, 0, 2).reshape(
        quarter, all_bins * CH
    )

    block = wide_index * seq_count + seq_index
    owners = lax.dynamic_slice_in_dim(session, block * quarter, quarter)
    same = owners[:, None] == owners[None, :]
    earlier = jnp.arange(quarter)[None, :] < jnp.arange(quarter)[:, None]
    rank = jnp.sum((same & earlier).astype(jnp.int32), axis=1)
    slot = owners * CAP + rank
    slot_count = wide_count * CAP
    dispatch = (jnp.arange(slot_count, dtype=jnp.int32)[:, None] == slot[None, :]).astype(
        jnp.bfloat16
    )
    outgoing = jnp.dot(dispatch, block_rows, preferred_element_type=jnp.float32).astype(
        jnp.bfloat16
    )
    arrived = lax.all_to_all(outgoing, "wide", split_axis=0, concat_axis=0, tiled=True)
    weight_block = readin_weight[0]
    merged = jnp.dot(weight_block, qkv_weight, preferred_element_type=jnp.float32)
    merged_hi = merged.astype(jnp.bfloat16)
    merged_lo = (merged - merged_hi.astype(jnp.float32)).astype(jnp.bfloat16)
    rows = arrived.reshape(slot_count * all_bins, CH)
    projected = jnp.dot(rows, merged_hi, preferred_element_type=jnp.float32) + jnp.dot(
        rows, merged_lo, preferred_element_type=jnp.float32
    )
    projected = projected.astype(jnp.bfloat16).reshape(slot_count, all_bins, qkv_weight.shape[1])
    weights = attention_weights(projected.reshape(slot_count * all_bins, qkv_weight.shape[1]))
    weights = weights.astype(jnp.bfloat16).reshape(slot_count, all_bins * HEADS * BINS)
    values = projected[:, :, (HEADS + KVH) * HD :].reshape(slot_count, all_bins * KVH * HD)
    payload = jnp.concatenate([values, weights], axis=1)
    returned = lax.all_to_all(payload, "wide", split_axis=0, concat_axis=0, tiled=True)
    mine = jnp.dot(dispatch.T, returned, preferred_element_type=jnp.float32).astype(jnp.bfloat16)
    split = all_bins * KVH * HD
    return heads_from(
        mine[:, split:].reshape(quarter, all_bins, HEADS * BINS),
        mine[:, :split].reshape(quarter, all_bins, KVH * HD),
    )


def solution(mesh):
    placed = (P("seq", "wide"), P("seq"), P(), P("wide", None, None), P())
    return jax.shard_map(
        body, mesh=mesh, in_specs=placed, out_specs=P(("wide", "seq"), None, None), check_vma=False
    )
```

```python
import jax
import jax.numpy as jnp
from jax import lax
from jax.experimental import pallas as pl
from jax.experimental.pallas import tpu as pltpu
from jax.sharding import PartitionSpec as P

CH = 128
HD = 128
HEADS = 8
KVH = 2
SPB = 20
CAP = 2
BINS = 8
ROWS = 128
SUB = 4


def _owner_kernel(rows_ref, hi_ref, lo_ref, o_ref, w_ref):
    group_size = HEADS // KVH
    sub_rows = SUB * BINS
    cols = SUB * group_size * BINS
    value_width = KVH * HD
    rows = rows_ref[...]
    projected = jnp.dot(rows, hi_ref[...], preferred_element_type=jnp.float32) + jnp.dot(
        rows, lo_ref[...], preferred_element_type=jnp.float32
    )
    projected = projected.astype(jnp.bfloat16)
    o_ref[:, :value_width] = projected[:, (HEADS + KVH) * HD :]
    projected = projected.astype(jnp.float32)
    row_patch = lax.broadcasted_iota(jnp.int32, (sub_rows, cols), 0) // BINS
    col_patch = lax.broadcasted_iota(jnp.int32, (sub_rows, cols), 1) // (group_size * BINS)
    same = row_patch == col_patch
    for sg in range(rows_ref.shape[0] // sub_rows):
        base = sg * sub_rows
        xs = projected[base : base + sub_rows, :]
        for g in range(KVH):
            k = xs[:, (HEADS + g) * HD : (HEADS + g + 1) * HD]
            k = k / jnp.sqrt(jnp.mean(k * k, axis=-1, keepdims=True) + 1e-06)
            pieces = []
            for p in range(SUB):
                for r in range(group_size):
                    h = g * group_size + r
                    pieces.append(xs[p * BINS : (p + 1) * BINS, h * HD : (h + 1) * HD])
            q = jnp.concatenate(pieces, axis=0)
            q = q / jnp.sqrt(jnp.mean(q * q, axis=-1, keepdims=True) + 1e-06)
            s = lax.dot_general(
                k, q, (((1,), (1,)), ((), ())), precision=lax.Precision.HIGHEST,
                preferred_element_type=jnp.float32,
            ) / HD**0.5
            e = jnp.where(same, jnp.exp(s), 0.0)
            w = (e / jnp.sum(e, axis=0, keepdims=True)).astype(jnp.bfloat16).astype(jnp.float32)
            width = group_size * BINS
            for p in range(SUB):
                tile = w[p * BINS : (p + 1) * BINS, :]
                compact = tile[:, 0:width]
                for c in range(1, SUB):
                    compact = compact + tile[:, c * width : (c + 1) * width]
                row0 = base + p * BINS
                w_ref[row0 : row0 + BINS, g * width : (g + 1) * width] = compact
    o_ref[:, value_width:] = w_ref[...].astype(jnp.bfloat16)


def owner_payload(rows, merged_hi, merged_lo):
    total, depth = rows.shape
    width = merged_hi.shape[1]
    return pl.pallas_call(
        _owner_kernel,
        out_shape=jax.ShapeDtypeStruct((total, KVH * HD + HEADS * BINS), jnp.bfloat16),
        grid=(total // ROWS,),
        in_specs=[
            pl.BlockSpec((ROWS, depth), lambda i: (i, 0)),
            pl.BlockSpec((depth, width), lambda i: (0, 0)),
            pl.BlockSpec((depth, width), lambda i: (0, 0)),
        ],
        out_specs=pl.BlockSpec((ROWS, KVH * HD + HEADS * BINS), lambda i: (i, 0)),
        scratch_shapes=[pltpu.VMEM((ROWS, HEADS * BINS), jnp.float32)],
    )(rows, merged_hi, merged_lo)


def heads_from(payload):
    n = payload.shape[0]
    group_size = HEADS // KVH
    v = payload[:, :, : KVH * HD].reshape(n, BINS, KVH, HD)
    w = payload[:, :, KVH * HD :].reshape(n, BINS, KVH, group_size, BINS)
    mixed = jnp.einsum("pjgri,pjge->pigre", w, v, preferred_element_type=jnp.float32)
    return mixed.reshape(n, BINS, HEADS * HD).astype(jnp.bfloat16)


def body(power, bin_index, session, readin_weight, qkv_weight):
    wide_count = lax.axis_size("wide")
    seq_count = lax.axis_size("seq")
    wide_index = lax.axis_index("wide")
    seq_index = lax.axis_index("seq")
    sample_rows, channels = power.shape
    patch_count = channels // CH
    quarter = patch_count // seq_count
    bin_count = sample_rows // SPB
    all_bins = bin_count * seq_count

    signal = power.astype(jnp.float32)
    partial = jnp.sum(signal * signal, axis=0)
    spread = jnp.broadcast_to(partial[None, :], (seq_count, channels))
    gathered = lax.all_to_all(spread, "seq", split_axis=0, concat_axis=0, tiled=True)
    squares = jnp.sum(gathered, axis=0)
    inv_rms = 1.0 / jnp.sqrt(squares / (sample_rows * seq_count) + 1e-06)
    active = jnp.maximum(signal * inv_rms[None, :] - 0.8, 0.0)
    local_bins = bin_index - seq_index * bin_count
    onehot = (local_bins[:, None] == jnp.arange(bin_count, dtype=jnp.int32)[None, :]).astype(
        jnp.float32
    )
    binned = (jnp.dot(onehot.T, active, precision=lax.Precision.HIGHEST) * (1.0 / SPB)).astype(
        jnp.bfloat16
    )
    binned = binned.reshape(bin_count, seq_count, quarter, CH).transpose(1, 0, 2, 3)
    binned = lax.all_to_all(binned, "seq", split_axis=0, concat_axis=0, tiled=True)
    block_rows = binned.reshape(all_bins, quarter, CH).transpose(1, 0, 2).reshape(
        quarter, all_bins * CH
    )

    block = wide_index * seq_count + seq_index
    owners = lax.dynamic_slice_in_dim(session, block * quarter, quarter)
    same = owners[:, None] == owners[None, :]
    earlier = jnp.arange(quarter)[None, :] < jnp.arange(quarter)[:, None]
    rank = jnp.sum((same & earlier).astype(jnp.int32), axis=1)
    slot = owners * CAP + rank
    slot_count = wide_count * CAP
    dispatch = (jnp.arange(slot_count, dtype=jnp.int32)[:, None] == slot[None, :]).astype(
        jnp.bfloat16
    )
    outgoing = jnp.dot(dispatch, block_rows, preferred_element_type=jnp.float32).astype(
        jnp.bfloat16
    )
    arrived = lax.all_to_all(outgoing, "wide", split_axis=0, concat_axis=0, tiled=True)
    weight_block = readin_weight[0]
    merged = jnp.dot(weight_block, qkv_weight, preferred_element_type=jnp.float32)
    merged_hi = merged.astype(jnp.bfloat16)
    merged_lo = (merged - merged_hi.astype(jnp.float32)).astype(jnp.bfloat16)
    rows = arrived.reshape(slot_count * all_bins, CH)
    payload = owner_payload(rows, merged_hi, merged_lo).reshape(slot_count, -1)
    returned = lax.all_to_all(payload, "wide", split_axis=0, concat_axis=0, tiled=True)
    mine = jnp.dot(dispatch.T, returned, preferred_element_type=jnp.float32).astype(jnp.bfloat16)
    return heads_from(mine.reshape(quarter, all_bins, -1))


def solution(mesh):
    placed = (P("seq", "wide"), P("seq"), P(), P("wide", None, None), P())
    return jax.shard_map(
        body, mesh=mesh, in_specs=placed, out_specs=P(("wide", "seq"), None, None), check_vma=False
    )
```

```python
import jax
import jax.numpy as jnp
from jax import lax
from jax.experimental import pallas as pl
from jax.experimental.pallas import tpu as pltpu
from jax.sharding import PartitionSpec as P

CH = 128
HD = 128
HEADS = 8
KVH = 2
SPB = 20
CAP = 2
BINS = 8
ROWS = 128
SUB = 4


def _owner_kernel(rows_ref, hi_ref, lo_ref, o_ref, w_ref):
    group_size = HEADS // KVH
    sub_rows = SUB * BINS
    cols = SUB * group_size * BINS
    value_width = KVH * HD
    rows = rows_ref[...]
    projected = jnp.dot(rows, hi_ref[...], preferred_element_type=jnp.float32) + jnp.dot(
        rows, lo_ref[...], preferred_element_type=jnp.float32
    )
    projected = projected.astype(jnp.bfloat16)
    o_ref[:, :value_width] = projected[:, (HEADS + KVH) * HD :]
    projected = projected.astype(jnp.float32)
    row_patch = lax.broadcasted_iota(jnp.int32, (sub_rows, cols), 0) // BINS
    col_patch = lax.broadcasted_iota(jnp.int32, (sub_rows, cols), 1) // (group_size * BINS)
    same = row_patch == col_patch
    for sg in range(rows_ref.shape[0] // sub_rows):
        base = sg * sub_rows
        xs = projected[base : base + sub_rows, :]
        for g in range(KVH):
            k = xs[:, (HEADS + g) * HD : (HEADS + g + 1) * HD]
            k = k / jnp.sqrt(jnp.mean(k * k, axis=-1, keepdims=True) + 1e-06)
            pieces = []
            for p in range(SUB):
                for r in range(group_size):
                    h = g * group_size + r
                    pieces.append(xs[p * BINS : (p + 1) * BINS, h * HD : (h + 1) * HD])
            q = jnp.concatenate(pieces, axis=0)
            q = q / jnp.sqrt(jnp.mean(q * q, axis=-1, keepdims=True) + 1e-06)
            s = lax.dot_general(
                k, q, (((1,), (1,)), ((), ())), precision=lax.Precision.HIGHEST,
                preferred_element_type=jnp.float32,
            ) / HD**0.5
            e = jnp.where(same, jnp.exp(s), 0.0)
            w = (e / jnp.sum(e, axis=0, keepdims=True)).astype(jnp.bfloat16).astype(jnp.float32)
            width = group_size * BINS
            for p in range(SUB):
                tile = w[p * BINS : (p + 1) * BINS, :]
                compact = tile[:, 0:width]
                for c in range(1, SUB):
                    compact = compact + tile[:, c * width : (c + 1) * width]
                row0 = base + p * BINS
                w_ref[row0 : row0 + BINS, g * width : (g + 1) * width] = compact
    o_ref[:, value_width:] = w_ref[...].astype(jnp.bfloat16)


def owner_payload(rows, merged_hi, merged_lo):
    total, depth = rows.shape
    width = merged_hi.shape[1]
    return pl.pallas_call(
        _owner_kernel,
        out_shape=jax.ShapeDtypeStruct((total, KVH * HD + HEADS * BINS), jnp.bfloat16),
        grid=(total // ROWS,),
        in_specs=[
            pl.BlockSpec((ROWS, depth), lambda i: (i, 0)),
            pl.BlockSpec((depth, width), lambda i: (0, 0)),
            pl.BlockSpec((depth, width), lambda i: (0, 0)),
        ],
        out_specs=pl.BlockSpec((ROWS, KVH * HD + HEADS * BINS), lambda i: (i, 0)),
        scratch_shapes=[pltpu.VMEM((ROWS, HEADS * BINS), jnp.float32)],
    )(rows, merged_hi, merged_lo)


def heads_from(payload):
    n = payload.shape[0]
    group_size = HEADS // KVH
    v = payload[:, :, : KVH * HD].reshape(n, BINS, KVH, HD)
    w = payload[:, :, KVH * HD :].reshape(n, BINS, KVH, group_size, BINS)
    mixed = jnp.einsum("pjgri,pjge->pigre", w, v, preferred_element_type=jnp.float32)
    return mixed.reshape(n, BINS, HEADS * HD).astype(jnp.bfloat16)


def body(power, bin_index, session, readin_weight, qkv_weight):
    wide_count = lax.axis_size("wide")
    seq_count = lax.axis_size("seq")
    wide_index = lax.axis_index("wide")
    seq_index = lax.axis_index("seq")
    sample_rows, channels = power.shape
    patch_count = channels // CH
    quarter = patch_count // seq_count
    bin_count = sample_rows // SPB
    all_bins = bin_count * seq_count

    signal = power.astype(jnp.float32)
    partial = jnp.sum(signal * signal, axis=0)
    squares = partial
    step = 1
    while step < seq_count:
        pairs = [(i, i ^ step) for i in range(seq_count)]
        squares = squares + lax.ppermute(squares, "seq", pairs)
        step *= 2
    inv_rms = 1.0 / jnp.sqrt(squares / (sample_rows * seq_count) + 1e-06)
    active = jnp.maximum(signal * inv_rms[None, :] - 0.8, 0.0)
    local_bins = bin_index - seq_index * bin_count
    onehot = (local_bins[:, None] == jnp.arange(bin_count, dtype=jnp.int32)[None, :]).astype(
        jnp.float32
    )
    binned = (jnp.dot(onehot.T, active, precision=lax.Precision.HIGHEST) * (1.0 / SPB)).astype(
        jnp.bfloat16
    )
    binned = binned.reshape(bin_count, seq_count, quarter, CH).transpose(1, 0, 2, 3)
    received = [lax.dynamic_index_in_dim(binned, seq_index, 0, keepdims=False)]
    for shift in range(1, seq_count):
        pairs = [(i, (i + shift) % seq_count) for i in range(seq_count)]
        piece = lax.dynamic_index_in_dim(binned, (seq_index + shift) % seq_count, 0, keepdims=False)
        received.append(lax.ppermute(piece, "seq", pairs))
    order = (seq_index - jnp.arange(seq_count, dtype=jnp.int32)) % seq_count
    binned = jnp.take(jnp.stack(received), order, axis=0)
    block_rows = binned.reshape(all_bins, quarter, CH).transpose(1, 0, 2).reshape(
        quarter, all_bins * CH
    )

    block = wide_index * seq_count + seq_index
    owners = lax.dynamic_slice_in_dim(session, block * quarter, quarter)
    same = owners[:, None] == owners[None, :]
    earlier = jnp.arange(quarter)[None, :] < jnp.arange(quarter)[:, None]
    rank = jnp.sum((same & earlier).astype(jnp.int32), axis=1)
    slot = owners * CAP + rank
    slot_count = wide_count * CAP
    dispatch = (jnp.arange(slot_count, dtype=jnp.int32)[:, None] == slot[None, :]).astype(
        jnp.bfloat16
    )
    outgoing = jnp.dot(dispatch, block_rows, preferred_element_type=jnp.float32).astype(
        jnp.bfloat16
    )
    arrived = lax.all_to_all(outgoing, "wide", split_axis=0, concat_axis=0, tiled=True)
    weight_block = readin_weight[0]
    merged = jnp.dot(weight_block, qkv_weight, preferred_element_type=jnp.float32)
    merged_hi = merged.astype(jnp.bfloat16)
    merged_lo = (merged - merged_hi.astype(jnp.float32)).astype(jnp.bfloat16)
    rows = arrived.reshape(slot_count * all_bins, CH)
    payload = owner_payload(rows, merged_hi, merged_lo).reshape(slot_count, -1)
    returned = lax.all_to_all(payload, "wide", split_axis=0, concat_axis=0, tiled=True)
    mine = jnp.dot(dispatch.T, returned, preferred_element_type=jnp.float32).astype(jnp.bfloat16)
    return heads_from(mine.reshape(quarter, all_bins, -1))


def solution(mesh):
    placed = (P("seq", "wide"), P("seq"), P(), P("wide", None, None), P())
    return jax.shard_map(
        body, mesh=mesh, in_specs=placed, out_specs=P(("wide", "seq"), None, None), check_vma=False
    )
```

```python
import jax
import jax.numpy as jnp
from jax import lax
from jax.experimental import pallas as pl
from jax.experimental.pallas import tpu as pltpu
from jax.sharding import PartitionSpec as P

CH = 128
HD = 128
HEADS = 8
KVH = 2
SPB = 20
CAP = 2
BINS = 8
ROWS = 128
SUB = 4


def _owner_kernel(rows_ref, hi_ref, lo_ref, o_ref, w_ref):
    group_size = HEADS // KVH
    sub_rows = SUB * BINS
    cols = SUB * group_size * BINS
    value_width = KVH * HD
    rows = rows_ref[...]
    projected = jnp.dot(rows, hi_ref[...], preferred_element_type=jnp.float32) + jnp.dot(
        rows, lo_ref[...], preferred_element_type=jnp.float32
    )
    projected = projected.astype(jnp.bfloat16)
    o_ref[:, :value_width] = projected[:, (HEADS + KVH) * HD :]
    projected = projected.astype(jnp.float32)
    row_patch = lax.broadcasted_iota(jnp.int32, (sub_rows, cols), 0) // BINS
    col_patch = lax.broadcasted_iota(jnp.int32, (sub_rows, cols), 1) // (group_size * BINS)
    same = row_patch == col_patch
    for sg in range(rows_ref.shape[0] // sub_rows):
        base = sg * sub_rows
        xs = projected[base : base + sub_rows, :]
        for g in range(KVH):
            k = xs[:, (HEADS + g) * HD : (HEADS + g + 1) * HD]
            k = k / jnp.sqrt(jnp.mean(k * k, axis=-1, keepdims=True) + 1e-06)
            pieces = []
            for p in range(SUB):
                for r in range(group_size):
                    h = g * group_size + r
                    pieces.append(xs[p * BINS : (p + 1) * BINS, h * HD : (h + 1) * HD])
            q = jnp.concatenate(pieces, axis=0)
            q = q / jnp.sqrt(jnp.mean(q * q, axis=-1, keepdims=True) + 1e-06)
            s = lax.dot_general(
                k, q, (((1,), (1,)), ((), ())), precision=lax.Precision.HIGHEST,
                preferred_element_type=jnp.float32,
            ) / HD**0.5
            e = jnp.where(same, jnp.exp(s), 0.0)
            w = (e / jnp.sum(e, axis=0, keepdims=True)).astype(jnp.bfloat16).astype(jnp.float32)
            width = group_size * BINS
            for p in range(SUB):
                tile = w[p * BINS : (p + 1) * BINS, :]
                compact = tile[:, 0:width]
                for c in range(1, SUB):
                    compact = compact + tile[:, c * width : (c + 1) * width]
                row0 = base + p * BINS
                w_ref[row0 : row0 + BINS, g * width : (g + 1) * width] = compact
    o_ref[:, value_width:] = w_ref[...].astype(jnp.bfloat16)


def owner_payload(rows, merged_hi, merged_lo):
    total, depth = rows.shape
    width = merged_hi.shape[1]
    return pl.pallas_call(
        _owner_kernel,
        out_shape=jax.ShapeDtypeStruct((total, KVH * HD + HEADS * BINS), jnp.bfloat16),
        grid=(total // ROWS,),
        in_specs=[
            pl.BlockSpec((ROWS, depth), lambda i: (i, 0)),
            pl.BlockSpec((depth, width), lambda i: (0, 0)),
            pl.BlockSpec((depth, width), lambda i: (0, 0)),
        ],
        out_specs=pl.BlockSpec((ROWS, KVH * HD + HEADS * BINS), lambda i: (i, 0)),
        scratch_shapes=[pltpu.VMEM((ROWS, HEADS * BINS), jnp.float32)],
    )(rows, merged_hi, merged_lo)


def heads_from(payload):
    n = payload.shape[0]
    group_size = HEADS // KVH
    v = payload[:, :, : KVH * HD].reshape(n, BINS, KVH, HD)
    w = payload[:, :, KVH * HD :].reshape(n, BINS, KVH, group_size, BINS)
    mixed = jnp.einsum("pjgri,pjge->pigre", w, v, preferred_element_type=jnp.float32)
    return mixed.reshape(n, BINS, HEADS * HD).astype(jnp.bfloat16)


WIDE_AXES = ("y", "z", "core")


def wide_all_to_all(x, sizes):
    ny, nz, nc = sizes
    total = x.shape[0]
    rest = (total // (ny * nz * nc),) + x.shape[1:]
    x = x.reshape(ny, nz, nc, *rest)
    x = lax.all_to_all(x, "z", split_axis=1, concat_axis=1, tiled=True)
    x = jnp.moveaxis(x, 2, 1).reshape(ny * nc, nz, *rest)
    x = lax.all_to_all(x, ("y", "core"), split_axis=0, concat_axis=0, tiled=True)
    x = jnp.moveaxis(x.reshape(ny, nc, nz, *rest), 1, 2)
    return x.reshape(total, *x.shape[4:])


def body(power, bin_index, session, readin_weight, qkv_weight):
    sizes = tuple(lax.axis_size(name) for name in WIDE_AXES)
    wide_count = sizes[0] * sizes[1] * sizes[2]
    seq_count = lax.axis_size("seq")
    wide_index = (lax.axis_index("y") * sizes[1] + lax.axis_index("z")) * sizes[2] + lax.axis_index(
        "core"
    )
    seq_index = lax.axis_index("seq")
    sample_rows, channels = power.shape
    patch_count = channels // CH
    quarter = patch_count // seq_count
    bin_count = sample_rows // SPB
    all_bins = bin_count * seq_count

    signal = power.astype(jnp.float32)
    partial = jnp.sum(signal * signal, axis=0)
    squares = partial
    step = 1
    while step < seq_count:
        pairs = [(i, i ^ step) for i in range(seq_count)]
        squares = squares + lax.ppermute(squares, "seq", pairs)
        step *= 2
    inv_rms = 1.0 / jnp.sqrt(squares / (sample_rows * seq_count) + 1e-06)
    active = jnp.maximum(signal * inv_rms[None, :] - 0.8, 0.0)
    local_bins = bin_index - seq_index * bin_count
    onehot = (local_bins[:, None] == jnp.arange(bin_count, dtype=jnp.int32)[None, :]).astype(
        jnp.float32
    )
    binned = (jnp.dot(onehot.T, active, precision=lax.Precision.HIGHEST) * (1.0 / SPB)).astype(
        jnp.bfloat16
    )
    binned = binned.reshape(bin_count, seq_count, quarter, CH).transpose(1, 0, 2, 3)
    received = [lax.dynamic_index_in_dim(binned, seq_index, 0, keepdims=False)]
    for shift in range(1, seq_count):
        pairs = [(i, (i + shift) % seq_count) for i in range(seq_count)]
        piece = lax.dynamic_index_in_dim(binned, (seq_index + shift) % seq_count, 0, keepdims=False)
        received.append(lax.ppermute(piece, "seq", pairs))
    order = (seq_index - jnp.arange(seq_count, dtype=jnp.int32)) % seq_count
    binned = jnp.take(jnp.stack(received), order, axis=0)
    block_rows = binned.reshape(all_bins, quarter, CH).transpose(1, 0, 2).reshape(
        quarter, all_bins * CH
    )

    block = wide_index * seq_count + seq_index
    owners = lax.dynamic_slice_in_dim(session, block * quarter, quarter)
    same = owners[:, None] == owners[None, :]
    earlier = jnp.arange(quarter)[None, :] < jnp.arange(quarter)[:, None]
    rank = jnp.sum((same & earlier).astype(jnp.int32), axis=1)
    slot = owners * CAP + rank
    slot_count = wide_count * CAP
    dispatch = (jnp.arange(slot_count, dtype=jnp.int32)[:, None] == slot[None, :]).astype(
        jnp.bfloat16
    )
    outgoing = jnp.dot(dispatch, block_rows, preferred_element_type=jnp.float32).astype(
        jnp.bfloat16
    )
    arrived = wide_all_to_all(outgoing, sizes)
    weight_block = readin_weight[0]
    merged = jnp.dot(weight_block, qkv_weight, preferred_element_type=jnp.float32)
    merged_hi = merged.astype(jnp.bfloat16)
    merged_lo = (merged - merged_hi.astype(jnp.float32)).astype(jnp.bfloat16)
    rows = arrived.reshape(slot_count * all_bins, CH)
    payload = owner_payload(rows, merged_hi, merged_lo).reshape(slot_count, -1)
    returned = wide_all_to_all(payload, sizes)
    mine = jnp.dot(dispatch.T, returned, preferred_element_type=jnp.float32).astype(jnp.bfloat16)
    return heads_from(mine.reshape(quarter, all_bins, -1))


def solution(mesh):
    sizes = (4, 8, 2)
    wide_total, seq_total = mesh.devices.shape
    assert sizes[0] * sizes[1] * sizes[2] == wide_total
    split = jax.sharding.Mesh(mesh.devices.reshape(*sizes, seq_total), WIDE_AXES + ("seq",))
    placed = (P("seq", WIDE_AXES), P("seq"), P(), P(WIDE_AXES, None, None), P())
    return jax.shard_map(
        body, mesh=split, in_specs=placed, out_specs=P(WIDE_AXES + ("seq",), None, None),
        check_vma=False,
    )
```

```python
import jax
import jax.numpy as jnp
from jax import lax
from jax.experimental import pallas as pl
from jax.experimental.pallas import tpu as pltpu
from jax.sharding import PartitionSpec as P

CH = 128
HD = 128
HEADS = 8
KVH = 2
SPB = 20
CAP = 2
BINS = 8
ROWS = 128
SUB = 4


def _owner_kernel(rows_ref, hi_ref, lo_ref, o_ref, w_ref):
    group_size = HEADS // KVH
    sub_rows = SUB * BINS
    cols = SUB * group_size * BINS
    value_width = KVH * HD
    rows = rows_ref[...]
    projected = jnp.dot(rows, hi_ref[...], preferred_element_type=jnp.float32) + jnp.dot(
        rows, lo_ref[...], preferred_element_type=jnp.float32
    )
    projected = projected.astype(jnp.bfloat16)
    o_ref[:, :value_width] = projected[:, (HEADS + KVH) * HD :]
    projected = projected.astype(jnp.float32)
    row_patch = lax.broadcasted_iota(jnp.int32, (sub_rows, cols), 0) // BINS
    col_patch = lax.broadcasted_iota(jnp.int32, (sub_rows, cols), 1) // (group_size * BINS)
    same = row_patch == col_patch
    for sg in range(rows_ref.shape[0] // sub_rows):
        base = sg * sub_rows
        xs = projected[base : base + sub_rows, :]
        for g in range(KVH):
            k = xs[:, (HEADS + g) * HD : (HEADS + g + 1) * HD]
            k = k / jnp.sqrt(jnp.mean(k * k, axis=-1, keepdims=True) + 1e-06)
            pieces = []
            for p in range(SUB):
                for r in range(group_size):
                    h = g * group_size + r
                    pieces.append(xs[p * BINS : (p + 1) * BINS, h * HD : (h + 1) * HD])
            q = jnp.concatenate(pieces, axis=0)
            q = q / jnp.sqrt(jnp.mean(q * q, axis=-1, keepdims=True) + 1e-06)
            s = lax.dot_general(
                k, q, (((1,), (1,)), ((), ())), precision=lax.Precision.HIGHEST,
                preferred_element_type=jnp.float32,
            ) / HD**0.5
            e = jnp.where(same, jnp.exp(s), 0.0)
            w = (e / jnp.sum(e, axis=0, keepdims=True)).astype(jnp.bfloat16).astype(jnp.float32)
            width = group_size * BINS
            for p in range(SUB):
                tile = w[p * BINS : (p + 1) * BINS, :]
                compact = tile[:, 0:width]
                for c in range(1, SUB):
                    compact = compact + tile[:, c * width : (c + 1) * width]
                row0 = base + p * BINS
                w_ref[row0 : row0 + BINS, g * width : (g + 1) * width] = compact
    o_ref[:, value_width:] = w_ref[...].astype(jnp.bfloat16)


def owner_payload(rows, merged_hi, merged_lo):
    total, depth = rows.shape
    width = merged_hi.shape[1]
    return pl.pallas_call(
        _owner_kernel,
        out_shape=jax.ShapeDtypeStruct((total, KVH * HD + HEADS * BINS), jnp.bfloat16),
        grid=(total // ROWS,),
        in_specs=[
            pl.BlockSpec((ROWS, depth), lambda i: (i, 0)),
            pl.BlockSpec((depth, width), lambda i: (0, 0)),
            pl.BlockSpec((depth, width), lambda i: (0, 0)),
        ],
        out_specs=pl.BlockSpec((ROWS, KVH * HD + HEADS * BINS), lambda i: (i, 0)),
        scratch_shapes=[pltpu.VMEM((ROWS, HEADS * BINS), jnp.float32)],
    )(rows, merged_hi, merged_lo)


def heads_from(payload):
    n = payload.shape[0]
    group_size = HEADS // KVH
    v = payload[:, :, : KVH * HD].reshape(n, BINS, KVH, HD)
    w = payload[:, :, KVH * HD :].reshape(n, BINS, KVH, group_size, BINS)
    mixed = jnp.einsum("pjgri,pjge->pigre", w, v, preferred_element_type=jnp.float32)
    return mixed.reshape(n, BINS, HEADS * HD).astype(jnp.bfloat16)


def body(power, bin_index, session, readin_weight, qkv_weight):
    wide_count = lax.axis_size("wide")
    seq_count = lax.axis_size("seq")
    wide_index = lax.axis_index("wide")
    seq_index = lax.axis_index("seq")
    sample_rows, channels = power.shape
    patch_count = channels // CH
    quarter = patch_count // seq_count
    bin_count = sample_rows // SPB
    all_bins = bin_count * seq_count

    signal = power.astype(jnp.float32)
    partial = jnp.sum(signal * signal, axis=0)
    received = [partial]
    for shift in range(1, seq_count):
        pairs = [(i, (i + shift) % seq_count) for i in range(seq_count)]
        received.append(lax.ppermute(partial, "seq", pairs))
    order = (seq_index - jnp.arange(seq_count, dtype=jnp.int32)) % seq_count
    squares = jnp.sum(jnp.take(jnp.stack(received), order, axis=0), axis=0)
    inv_rms = 1.0 / jnp.sqrt(squares / (sample_rows * seq_count) + 1e-06)
    active = jnp.maximum(signal * inv_rms[None, :] - 0.8, 0.0)
    local_bins = bin_index - seq_index * bin_count
    onehot = (local_bins[:, None] == jnp.arange(bin_count, dtype=jnp.int32)[None, :]).astype(
        jnp.float32
    )
    binned = (jnp.dot(onehot.T, active, precision=lax.Precision.HIGHEST) * (1.0 / SPB)).astype(
        jnp.bfloat16
    )
    binned = binned.reshape(bin_count, seq_count, quarter, CH).transpose(1, 0, 2, 3)
    received = [lax.dynamic_index_in_dim(binned, seq_index, 0, keepdims=False)]
    for shift in range(1, seq_count):
        pairs = [(i, (i + shift) % seq_count) for i in range(seq_count)]
        piece = lax.dynamic_index_in_dim(binned, (seq_index + shift) % seq_count, 0, keepdims=False)
        received.append(lax.ppermute(piece, "seq", pairs))
    order = (seq_index - jnp.arange(seq_count, dtype=jnp.int32)) % seq_count
    binned = jnp.take(jnp.stack(received), order, axis=0)
    block_rows = binned.reshape(all_bins, quarter, CH).transpose(1, 0, 2).reshape(
        quarter, all_bins * CH
    )

    block = wide_index * seq_count + seq_index
    owners = lax.dynamic_slice_in_dim(session, block * quarter, quarter)
    same = owners[:, None] == owners[None, :]
    earlier = jnp.arange(quarter)[None, :] < jnp.arange(quarter)[:, None]
    rank = jnp.sum((same & earlier).astype(jnp.int32), axis=1)
    slot = owners * CAP + rank
    slot_count = wide_count * CAP
    dispatch = (jnp.arange(slot_count, dtype=jnp.int32)[:, None] == slot[None, :]).astype(
        jnp.bfloat16
    )
    outgoing = jnp.dot(dispatch, block_rows, preferred_element_type=jnp.float32).astype(
        jnp.bfloat16
    )
    arrived = lax.all_to_all(outgoing, "wide", split_axis=0, concat_axis=0, tiled=True)
    weight_block = readin_weight[0]
    merged = jnp.dot(weight_block, qkv_weight, preferred_element_type=jnp.float32)
    merged_hi = merged.astype(jnp.bfloat16)
    merged_lo = (merged - merged_hi.astype(jnp.float32)).astype(jnp.bfloat16)
    rows = arrived.reshape(slot_count * all_bins, CH)
    payload = owner_payload(rows, merged_hi, merged_lo).reshape(slot_count, -1)
    returned = lax.all_to_all(payload, "wide", split_axis=0, concat_axis=0, tiled=True)
    mine = jnp.dot(dispatch.T, returned, preferred_element_type=jnp.float32).astype(jnp.bfloat16)
    return heads_from(mine.reshape(quarter, all_bins, -1))


def solution(mesh):
    placed = (P("seq", "wide"), P("seq"), P(), P("wide", None, None), P())
    return jax.shard_map(
        body, mesh=mesh, in_specs=placed, out_specs=P(("wide", "seq"), None, None), check_vma=False
    )
```

```python
import jax
import jax.numpy as jnp
from jax import lax
from jax.experimental import pallas as pl
from jax.experimental.pallas import tpu as pltpu
from jax.sharding import PartitionSpec as P

CH = 128
HD = 128
HEADS = 8
KVH = 2
SPB = 20
CAP = 2
BINS = 8
ROWS = 128
SUB = 4


def _owner_kernel(rows_ref, hi_ref, lo_ref, o_ref, w_ref):
    group_size = HEADS // KVH
    sub_rows = SUB * BINS
    cols = SUB * group_size * BINS
    value_width = KVH * HD
    rows = rows_ref[...]
    projected = jnp.dot(rows, hi_ref[...], preferred_element_type=jnp.float32) + jnp.dot(
        rows, lo_ref[...], preferred_element_type=jnp.float32
    )
    projected = projected.astype(jnp.bfloat16)
    o_ref[:, :value_width] = projected[:, (HEADS + KVH) * HD :]
    row_patch = lax.broadcasted_iota(jnp.int32, (sub_rows, cols), 0) // BINS
    col_patch = lax.broadcasted_iota(jnp.int32, (sub_rows, cols), 1) // (group_size * BINS)
    same = row_patch == col_patch
    ones = jnp.ones((8, HD), jnp.float32)
    for sg in range(rows_ref.shape[0] // sub_rows):
        base = sg * sub_rows
        xs = projected[base : base + sub_rows, :]
        for g in range(KVH):
            k = xs[:, (HEADS + g) * HD : (HEADS + g + 1) * HD]
            kf = k.astype(jnp.float32)
            k_scale = 1.0 / jnp.sqrt(jnp.mean(kf * kf, axis=-1, keepdims=True) + 1e-06)
            pieces = []
            for p in range(SUB):
                for r in range(group_size):
                    h = g * group_size + r
                    pieces.append(xs[p * BINS : (p + 1) * BINS, h * HD : (h + 1) * HD])
            q = jnp.concatenate(pieces, axis=0)
            qf = q.astype(jnp.float32)
            q_sums = lax.dot_general(
                ones, qf * qf, (((1,), (1,)), ((), ())), precision=lax.Precision.HIGHEST,
                preferred_element_type=jnp.float32,
            )[0:1, :]
            q_scale = 1.0 / jnp.sqrt(q_sums / HD + 1e-06)
            raw = lax.dot_general(
                k, q, (((1,), (1,)), ((), ())), preferred_element_type=jnp.float32
            )
            s = raw * k_scale * q_scale / HD**0.5
            e = jnp.where(same, jnp.exp(s), 0.0)
            total = jnp.sum(e, axis=0, keepdims=True)
            w = (e * (1.0 / total)).astype(jnp.bfloat16).astype(jnp.float32)
            width = group_size * BINS
            for p in range(SUB):
                tile = w[p * BINS : (p + 1) * BINS, :]
                compact = tile[:, 0:width]
                for c in range(1, SUB):
                    compact = compact + tile[:, c * width : (c + 1) * width]
                row0 = base + p * BINS
                w_ref[row0 : row0 + BINS, g * width : (g + 1) * width] = compact
    o_ref[:, value_width:] = w_ref[...].astype(jnp.bfloat16)


def owner_payload(rows, merged_hi, merged_lo):
    total, depth = rows.shape
    width = merged_hi.shape[1]
    return pl.pallas_call(
        _owner_kernel,
        out_shape=jax.ShapeDtypeStruct((total, KVH * HD + HEADS * BINS), jnp.bfloat16),
        grid=(total // ROWS,),
        in_specs=[
            pl.BlockSpec((ROWS, depth), lambda i: (i, 0)),
            pl.BlockSpec((depth, width), lambda i: (0, 0)),
            pl.BlockSpec((depth, width), lambda i: (0, 0)),
        ],
        out_specs=pl.BlockSpec((ROWS, KVH * HD + HEADS * BINS), lambda i: (i, 0)),
        scratch_shapes=[pltpu.VMEM((ROWS, HEADS * BINS), jnp.float32)],
    )(rows, merged_hi, merged_lo)


def heads_from(payload):
    n = payload.shape[0]
    group_size = HEADS // KVH
    v = payload[:, :, : KVH * HD].reshape(n, BINS, KVH, HD)
    w = payload[:, :, KVH * HD :].reshape(n, BINS, KVH, group_size, BINS)
    mixed = jnp.einsum("pjgri,pjge->pigre", w, v, preferred_element_type=jnp.float32)
    return mixed.reshape(n, BINS, HEADS * HD).astype(jnp.bfloat16)


def body(power, bin_index, session, readin_weight, qkv_weight):
    wide_count = lax.axis_size("wide")
    seq_count = lax.axis_size("seq")
    wide_index = lax.axis_index("wide")
    seq_index = lax.axis_index("seq")
    sample_rows, channels = power.shape
    patch_count = channels // CH
    quarter = patch_count // seq_count
    bin_count = sample_rows // SPB
    all_bins = bin_count * seq_count

    signal = power.astype(jnp.float32)
    partial = jnp.sum(signal * signal, axis=0)
    received = [partial]
    for shift in range(1, seq_count):
        pairs = [(i, (i + shift) % seq_count) for i in range(seq_count)]
        received.append(lax.ppermute(partial, "seq", pairs))
    order = (seq_index - jnp.arange(seq_count, dtype=jnp.int32)) % seq_count
    squares = jnp.sum(jnp.take(jnp.stack(received), order, axis=0), axis=0)
    inv_rms = 1.0 / jnp.sqrt(squares / (sample_rows * seq_count) + 1e-06)
    active = jnp.maximum(signal * inv_rms[None, :] - 0.8, 0.0)
    local_bins = bin_index - seq_index * bin_count
    sums = [
        jnp.sum(jnp.where((local_bins == b)[:, None], active, 0.0), axis=0) for b in range(bin_count)
    ]
    binned = (jnp.stack(sums) * (1.0 / SPB)).astype(jnp.bfloat16)
    binned = binned.reshape(bin_count, seq_count, quarter, CH).transpose(1, 0, 2, 3)
    received = [lax.dynamic_index_in_dim(binned, seq_index, 0, keepdims=False)]
    for shift in range(1, seq_count):
        pairs = [(i, (i + shift) % seq_count) for i in range(seq_count)]
        piece = lax.dynamic_index_in_dim(binned, (seq_index + shift) % seq_count, 0, keepdims=False)
        received.append(lax.ppermute(piece, "seq", pairs))
    order = (seq_index - jnp.arange(seq_count, dtype=jnp.int32)) % seq_count
    binned = jnp.take(jnp.stack(received), order, axis=0)
    block_rows = binned.reshape(all_bins, quarter, CH).transpose(1, 0, 2).reshape(
        quarter, all_bins * CH
    )

    block = wide_index * seq_count + seq_index
    owners = lax.dynamic_slice_in_dim(session, block * quarter, quarter)
    same = owners[:, None] == owners[None, :]
    earlier = jnp.arange(quarter)[None, :] < jnp.arange(quarter)[:, None]
    rank = jnp.sum((same & earlier).astype(jnp.int32), axis=1)
    slot = owners * CAP + rank
    slot_count = wide_count * CAP
    dispatch = (jnp.arange(slot_count, dtype=jnp.int32)[:, None] == slot[None, :]).astype(
        jnp.bfloat16
    )
    outgoing = jnp.dot(dispatch, block_rows, preferred_element_type=jnp.float32).astype(
        jnp.bfloat16
    )
    arrived = lax.all_to_all(outgoing, "wide", split_axis=0, concat_axis=0, tiled=True)
    weight_block = readin_weight[0]
    merged = jnp.dot(weight_block, qkv_weight, preferred_element_type=jnp.float32)
    merged_hi = merged.astype(jnp.bfloat16)
    merged_lo = (merged - merged_hi.astype(jnp.float32)).astype(jnp.bfloat16)
    rows = arrived.reshape(slot_count * all_bins, CH)
    payload = owner_payload(rows, merged_hi, merged_lo).reshape(slot_count, -1)
    returned = lax.all_to_all(payload, "wide", split_axis=0, concat_axis=0, tiled=True)
    mine = jnp.dot(dispatch.T, returned, preferred_element_type=jnp.float32).astype(jnp.bfloat16)
    return heads_from(mine.reshape(quarter, all_bins, -1))


def solution(mesh):
    placed = (P("seq", "wide"), P("seq"), P(), P("wide", None, None), P())
    return jax.shard_map(
        body, mesh=mesh, in_specs=placed, out_specs=P(("wide", "seq"), None, None), check_vma=False
    )
```

```python
import jax
import jax.numpy as jnp
from jax import lax
from jax.experimental import pallas as pl
from jax.experimental.pallas import tpu as pltpu
from jax.sharding import PartitionSpec as P

CH = 128
HD = 128
HEADS = 8
KVH = 2
SPB = 20
CAP = 2
BINS = 8
ROWS = 128
SUB = 4


def _owner_kernel(rows_ref, hi_ref, lo_ref, o_ref, w_ref):
    group_size = HEADS // KVH
    sub_rows = SUB * BINS
    cols = SUB * group_size * BINS
    value_width = KVH * HD
    rows = rows_ref[...]
    projected = jnp.dot(rows, hi_ref[...], preferred_element_type=jnp.float32) + jnp.dot(
        rows, lo_ref[...], preferred_element_type=jnp.float32
    )
    projected = projected.astype(jnp.bfloat16)
    o_ref[:, :value_width] = projected[:, (HEADS + KVH) * HD :]
    row_patch = lax.broadcasted_iota(jnp.int32, (sub_rows, cols), 0) // BINS
    col_patch = lax.broadcasted_iota(jnp.int32, (sub_rows, cols), 1) // (group_size * BINS)
    same = row_patch == col_patch
    ones = jnp.ones((8, HD), jnp.float32)
    for sg in range(rows_ref.shape[0] // sub_rows):
        base = sg * sub_rows
        xs = projected[base : base + sub_rows, :]
        for g in range(KVH):
            k = xs[:, (HEADS + g) * HD : (HEADS + g + 1) * HD]
            kf = k.astype(jnp.float32)
            k_scale = 1.0 / jnp.sqrt(jnp.mean(kf * kf, axis=-1, keepdims=True) + 1e-06)
            pieces = []
            for p in range(SUB):
                for r in range(group_size):
                    h = g * group_size + r
                    pieces.append(xs[p * BINS : (p + 1) * BINS, h * HD : (h + 1) * HD])
            q = jnp.concatenate(pieces, axis=0)
            qf = q.astype(jnp.float32)
            q_sums = lax.dot_general(
                ones, qf * qf, (((1,), (1,)), ((), ())), precision=lax.Precision.HIGHEST,
                preferred_element_type=jnp.float32,
            )[0:1, :]
            q_scale = 1.0 / jnp.sqrt(q_sums / HD + 1e-06)
            raw = lax.dot_general(
                k, q, (((1,), (1,)), ((), ())), preferred_element_type=jnp.float32
            )
            s = raw * k_scale * q_scale / HD**0.5
            e = jnp.where(same, jnp.exp(s), 0.0)
            total = jnp.sum(e, axis=0, keepdims=True)
            w = (e * (1.0 / total)).astype(jnp.bfloat16).astype(jnp.float32)
            width = group_size * BINS
            for p in range(SUB):
                tile = w[p * BINS : (p + 1) * BINS, :]
                compact = tile[:, 0:width]
                for c in range(1, SUB):
                    compact = compact + tile[:, c * width : (c + 1) * width]
                row0 = base + p * BINS
                w_ref[row0 : row0 + BINS, g * width : (g + 1) * width] = compact
    o_ref[:, value_width:] = w_ref[...].astype(jnp.bfloat16)


def owner_payload(rows, merged_hi, merged_lo):
    total, depth = rows.shape
    width = merged_hi.shape[1]
    return pl.pallas_call(
        _owner_kernel,
        out_shape=jax.ShapeDtypeStruct((total, KVH * HD + HEADS * BINS), jnp.bfloat16),
        grid=(total // ROWS,),
        in_specs=[
            pl.BlockSpec((ROWS, depth), lambda i: (i, 0)),
            pl.BlockSpec((depth, width), lambda i: (0, 0)),
            pl.BlockSpec((depth, width), lambda i: (0, 0)),
        ],
        out_specs=pl.BlockSpec((ROWS, KVH * HD + HEADS * BINS), lambda i: (i, 0)),
        scratch_shapes=[pltpu.VMEM((ROWS, HEADS * BINS), jnp.float32)],
    )(rows, merged_hi, merged_lo)


def heads_from(payload):
    n = payload.shape[0]
    group_size = HEADS // KVH
    v = payload[:, :, : KVH * HD].reshape(n, BINS, KVH, HD)
    w = payload[:, :, KVH * HD :].reshape(n, BINS, KVH, group_size, BINS)
    mixed = jnp.einsum("pjgri,pjge->pigre", w, v, preferred_element_type=jnp.float32)
    return mixed.reshape(n, BINS, HEADS * HD).astype(jnp.bfloat16)


WIDE_AXES = ("y", "z", "core")


def relative_exchange(x, sizes):
    ny, nz, nc = sizes
    moved = [x[:, 0]]
    for d in range(1, nz):
        moved.append(lax.ppermute(x[:, d], "z", [(i, (i + d) % nz) for i in range(nz)]))
    x = jnp.stack(moved)
    moved = [x[:, 0]]
    for d in range(1, ny):
        moved.append(lax.ppermute(x[:, d], "y", [(i, (i + d) % ny) for i in range(ny)]))
    x = jnp.stack(moved)
    moved = [x[:, :, 0]]
    for d in range(1, nc):
        moved.append(lax.ppermute(x[:, :, d], "core", [(i, (i + d) % nc) for i in range(nc)]))
    return jnp.stack(moved)


def negate_offsets(x, axis):
    head = lax.slice_in_dim(x, 0, 1, axis=axis)
    tail = jnp.flip(lax.slice_in_dim(x, 1, x.shape[axis], axis=axis), axis=axis)
    return jnp.concatenate([head, tail], axis=axis)


def body(power, bin_index, session, readin_weight, qkv_weight):
    sizes = tuple(lax.axis_size(name) for name in WIDE_AXES)
    ny, nz, nc = sizes
    wide_count = ny * nz * nc
    seq_count = lax.axis_size("seq")
    my_y, my_z, my_c = (lax.axis_index(name) for name in WIDE_AXES)
    wide_index = (my_y * nz + my_z) * nc + my_c
    seq_index = lax.axis_index("seq")
    sample_rows, channels = power.shape
    patch_count = channels // CH
    quarter = patch_count // seq_count
    bin_count = sample_rows // SPB
    all_bins = bin_count * seq_count

    signal = power.astype(jnp.float32)
    partial = jnp.sum(signal * signal, axis=0)
    received = [partial]
    for shift in range(1, seq_count):
        pairs = [(i, (i + shift) % seq_count) for i in range(seq_count)]
        received.append(lax.ppermute(partial, "seq", pairs))
    order = (seq_index - jnp.arange(seq_count, dtype=jnp.int32)) % seq_count
    squares = jnp.sum(jnp.take(jnp.stack(received), order, axis=0), axis=0)
    inv_rms = 1.0 / jnp.sqrt(squares / (sample_rows * seq_count) + 1e-06)
    active = jnp.maximum(signal * inv_rms[None, :] - 0.8, 0.0)
    local_bins = bin_index - seq_index * bin_count
    sums = [
        jnp.sum(jnp.where((local_bins == b)[:, None], active, 0.0), axis=0) for b in range(bin_count)
    ]
    binned = (jnp.stack(sums) * (1.0 / SPB)).astype(jnp.bfloat16)
    binned = binned.reshape(bin_count, seq_count, quarter, CH).transpose(1, 0, 2, 3)
    received = [lax.dynamic_index_in_dim(binned, seq_index, 0, keepdims=False)]
    for shift in range(1, seq_count):
        pairs = [(i, (i + shift) % seq_count) for i in range(seq_count)]
        piece = lax.dynamic_index_in_dim(binned, (seq_index + shift) % seq_count, 0, keepdims=False)
        received.append(lax.ppermute(piece, "seq", pairs))
    order = (seq_index - jnp.arange(seq_count, dtype=jnp.int32)) % seq_count
    binned = jnp.take(jnp.stack(received), order, axis=0)
    block_rows = binned.reshape(all_bins, quarter, CH).transpose(1, 0, 2).reshape(
        quarter, all_bins * CH
    )

    block = wide_index * seq_count + seq_index
    owners = lax.dynamic_slice_in_dim(session, block * quarter, quarter)
    same = owners[:, None] == owners[None, :]
    earlier = jnp.arange(quarter)[None, :] < jnp.arange(quarter)[:, None]
    rank = jnp.sum((same & earlier).astype(jnp.int32), axis=1)
    owner_y = owners // (nz * nc)
    owner_z = (owners // nc) % nz
    owner_c = owners % nc
    ahead = (((owner_y - my_y) % ny) * nz + (owner_z - my_z) % nz) * nc + (owner_c - my_c) % nc
    behind = (((my_c - owner_c) % nc) * ny + (my_y - owner_y) % ny) * nz + (my_z - owner_z) % nz
    slot_count = wide_count * CAP
    slot_ids = jnp.arange(slot_count, dtype=jnp.int32)[:, None]
    dispatch = (slot_ids == (ahead * CAP + rank)[None, :]).astype(jnp.bfloat16)
    collect = (slot_ids == (behind * CAP + rank)[None, :]).astype(jnp.bfloat16)
    outgoing = jnp.dot(dispatch, block_rows, preferred_element_type=jnp.float32).astype(
        jnp.bfloat16
    )
    arrived = relative_exchange(outgoing.reshape(ny, nz, nc, CAP, -1), sizes)
    arrived = jnp.transpose(arrived, (1, 2, 0, 3, 4))
    for axis in range(3):
        arrived = negate_offsets(arrived, axis)
    weight_block = readin_weight[0]
    merged = jnp.dot(weight_block, qkv_weight, preferred_element_type=jnp.float32)
    merged_hi = merged.astype(jnp.bfloat16)
    merged_lo = (merged - merged_hi.astype(jnp.float32)).astype(jnp.bfloat16)
    rows = arrived.reshape(slot_count * all_bins, CH)
    payload = owner_payload(rows, merged_hi, merged_lo).reshape(slot_count, -1)
    returned = relative_exchange(payload.reshape(ny, nz, nc, CAP, -1), sizes)
    returned = returned.reshape(slot_count, -1)
    mine = jnp.dot(collect.T, returned, preferred_element_type=jnp.float32).astype(jnp.bfloat16)
    return heads_from(mine.reshape(quarter, all_bins, -1))


def solution(mesh):
    sizes = (4, 8, 2)
    wide_total, seq_total = mesh.devices.shape
    assert sizes[0] * sizes[1] * sizes[2] == wide_total
    split = jax.sharding.Mesh(mesh.devices.reshape(*sizes, seq_total), WIDE_AXES + ("seq",))
    placed = (P("seq", WIDE_AXES), P("seq"), P(), P(WIDE_AXES, None, None), P())
    return jax.shard_map(
        body, mesh=split, in_specs=placed, out_specs=P(WIDE_AXES + ("seq",), None, None),
        check_vma=False,
    )
```

```python
import jax
import jax.numpy as jnp
from jax import lax
from jax.experimental import pallas as pl
from jax.experimental.pallas import tpu as pltpu
from jax.sharding import PartitionSpec as P

CH = 128
HD = 128
HEADS = 8
KVH = 2
SPB = 20
CAP = 2
BINS = 8
ROWS = 128
SUB = 4


def _owner_kernel(rows_ref, hi_ref, lo_ref, o_ref, w_ref):
    group_size = HEADS // KVH
    sub_rows = SUB * BINS
    cols = SUB * group_size * BINS
    value_width = KVH * HD
    rows = rows_ref[...]
    projected = jnp.dot(rows, hi_ref[...], preferred_element_type=jnp.float32) + jnp.dot(
        rows, lo_ref[...], preferred_element_type=jnp.float32
    )
    projected = projected.astype(jnp.bfloat16)
    o_ref[:, :value_width] = projected[:, (HEADS + KVH) * HD :]
    row_patch = lax.broadcasted_iota(jnp.int32, (sub_rows, cols), 0) // BINS
    col_patch = lax.broadcasted_iota(jnp.int32, (sub_rows, cols), 1) // (group_size * BINS)
    same = row_patch == col_patch
    ones = jnp.ones((8, HD), jnp.bfloat16)
    for sg in range(rows_ref.shape[0] // sub_rows):
        base = sg * sub_rows
        xs = projected[base : base + sub_rows, :]
        for g in range(KVH):
            k = xs[:, (HEADS + g) * HD : (HEADS + g + 1) * HD]
            kf = k.astype(jnp.float32)
            k_scale = 1.0 / jnp.sqrt(jnp.mean(kf * kf, axis=-1, keepdims=True) + 1e-06)
            pieces = []
            for p in range(SUB):
                for r in range(group_size):
                    h = g * group_size + r
                    pieces.append(xs[p * BINS : (p + 1) * BINS, h * HD : (h + 1) * HD])
            q = jnp.concatenate(pieces, axis=0)
            qf = q.astype(jnp.float32)
            q2 = qf * qf
            q2_hi = q2.astype(jnp.bfloat16)
            q2_lo = (q2 - q2_hi.astype(jnp.float32)).astype(jnp.bfloat16)
            q_sums = lax.dot_general(
                ones, q2_hi, (((1,), (1,)), ((), ())), preferred_element_type=jnp.float32
            ) + lax.dot_general(
                ones, q2_lo, (((1,), (1,)), ((), ())), preferred_element_type=jnp.float32
            )
            q_sums = q_sums[0:1, :]
            q_scale = 1.0 / jnp.sqrt(q_sums / HD + 1e-06)
            raw = lax.dot_general(
                k, q, (((1,), (1,)), ((), ())), preferred_element_type=jnp.float32
            )
            s = raw * k_scale * q_scale / HD**0.5
            e = jnp.where(same, jnp.exp(s), 0.0)
            total = jnp.sum(e, axis=0, keepdims=True)
            w = (e * (1.0 / total)).astype(jnp.bfloat16).astype(jnp.float32)
            width = group_size * BINS
            for p in range(SUB):
                tile = w[p * BINS : (p + 1) * BINS, :]
                compact = tile[:, 0:width]
                for c in range(1, SUB):
                    compact = compact + tile[:, c * width : (c + 1) * width]
                row0 = base + p * BINS
                w_ref[row0 : row0 + BINS, g * width : (g + 1) * width] = compact
    o_ref[:, value_width:] = w_ref[...].astype(jnp.bfloat16)


def owner_payload(rows, merged_hi, merged_lo):
    total, depth = rows.shape
    width = merged_hi.shape[1]
    return pl.pallas_call(
        _owner_kernel,
        out_shape=jax.ShapeDtypeStruct((total, KVH * HD + HEADS * BINS), jnp.bfloat16),
        grid=(total // ROWS,),
        in_specs=[
            pl.BlockSpec((ROWS, depth), lambda i: (i, 0)),
            pl.BlockSpec((depth, width), lambda i: (0, 0)),
            pl.BlockSpec((depth, width), lambda i: (0, 0)),
        ],
        out_specs=pl.BlockSpec((ROWS, KVH * HD + HEADS * BINS), lambda i: (i, 0)),
        scratch_shapes=[pltpu.VMEM((ROWS, HEADS * BINS), jnp.float32)],
    )(rows, merged_hi, merged_lo)


def heads_from(payload):
    n = payload.shape[0]
    group_size = HEADS // KVH
    v = payload[:, :, : KVH * HD].reshape(n, BINS, KVH, HD)
    w = payload[:, :, KVH * HD :].reshape(n, BINS, KVH, group_size, BINS)
    mixed = jnp.einsum("pjgri,pjge->pigre", w, v, preferred_element_type=jnp.float32)
    return mixed.reshape(n, BINS, HEADS * HD).astype(jnp.bfloat16)


def body(power, bin_index, session, readin_weight, qkv_weight):
    wide_count = lax.axis_size("wide")
    seq_count = lax.axis_size("seq")
    wide_index = lax.axis_index("wide")
    seq_index = lax.axis_index("seq")
    sample_rows, channels = power.shape
    patch_count = channels // CH
    quarter = patch_count // seq_count
    bin_count = sample_rows // SPB
    all_bins = bin_count * seq_count

    signal = power.astype(jnp.float32)
    partial = jnp.sum(signal * signal, axis=0)
    received = [partial]
    for shift in range(1, seq_count):
        pairs = [(i, (i + shift) % seq_count) for i in range(seq_count)]
        received.append(lax.ppermute(partial, "seq", pairs))
    squares = received[0]
    for piece in received[1:]:
        squares = squares + piece
    inv_rms = 1.0 / jnp.sqrt(squares / (sample_rows * seq_count) + 1e-06)
    active = jnp.maximum(signal * inv_rms[None, :] - 0.8, 0.0)
    local_bins = bin_index - seq_index * bin_count
    sums = [
        jnp.sum(jnp.where((local_bins == b)[:, None], active, 0.0), axis=0) for b in range(bin_count)
    ]
    binned = (jnp.stack(sums) * (1.0 / SPB)).astype(jnp.bfloat16)
    binned = binned.reshape(bin_count, seq_count, quarter, CH).transpose(1, 0, 2, 3)
    received = [lax.dynamic_index_in_dim(binned, seq_index, 0, keepdims=False)]
    for shift in range(1, seq_count):
        pairs = [(i, (i + shift) % seq_count) for i in range(seq_count)]
        piece = lax.dynamic_index_in_dim(binned, (seq_index + shift) % seq_count, 0, keepdims=False)
        received.append(lax.ppermute(piece, "seq", pairs))
    order = (seq_index - jnp.arange(seq_count, dtype=jnp.int32)) % seq_count
    binned = jnp.take(jnp.stack(received), order, axis=0)
    block_rows = binned.reshape(all_bins, quarter, CH).transpose(1, 0, 2).reshape(
        quarter, all_bins * CH
    )

    block = wide_index * seq_count + seq_index
    owners = lax.dynamic_slice_in_dim(session, block * quarter, quarter)
    same = owners[:, None] == owners[None, :]
    earlier = jnp.arange(quarter)[None, :] < jnp.arange(quarter)[:, None]
    rank = jnp.sum((same & earlier).astype(jnp.int32), axis=1)
    slot = owners * CAP + rank
    slot_count = wide_count * CAP
    dispatch = (jnp.arange(slot_count, dtype=jnp.int32)[:, None] == slot[None, :]).astype(
        jnp.bfloat16
    )
    outgoing = jnp.dot(dispatch, block_rows, preferred_element_type=jnp.float32).astype(
        jnp.bfloat16
    )
    arrived = lax.all_to_all(outgoing, "wide", split_axis=0, concat_axis=0, tiled=True)
    weight_block = readin_weight[0]
    merged = jnp.dot(weight_block, qkv_weight, preferred_element_type=jnp.float32)
    merged_hi = merged.astype(jnp.bfloat16)
    merged_lo = (merged - merged_hi.astype(jnp.float32)).astype(jnp.bfloat16)
    rows = arrived.reshape(slot_count * all_bins, CH)
    payload = owner_payload(rows, merged_hi, merged_lo).reshape(slot_count, -1)
    returned = lax.all_to_all(payload, "wide", split_axis=0, concat_axis=0, tiled=True)
    mine = jnp.dot(dispatch.T, returned, preferred_element_type=jnp.float32).astype(jnp.bfloat16)
    return heads_from(mine.reshape(quarter, all_bins, -1))


def solution(mesh):
    placed = (P("seq", "wide"), P("seq"), P(), P("wide", None, None), P())
    return jax.shard_map(
        body, mesh=mesh, in_specs=placed, out_specs=P(("wide", "seq"), None, None), check_vma=False
    )
```

```python
import jax
import jax.numpy as jnp
from jax import lax
from jax.experimental import pallas as pl
from jax.experimental.pallas import tpu as pltpu
from jax.sharding import PartitionSpec as P

CH = 128
HD = 128
HEADS = 8
KVH = 2
SPB = 20
CAP = 2
BINS = 8
ROWS = 128
SUB = 4


def _owner_kernel(rows_ref, hi_ref, lo_ref, o_ref, w_ref):
    group_size = HEADS // KVH
    sub_rows = SUB * BINS
    cols = SUB * group_size * BINS
    value_width = KVH * HD
    rows = rows_ref[...]
    projected = jnp.dot(rows, hi_ref[...], preferred_element_type=jnp.float32) + jnp.dot(
        rows, lo_ref[...], preferred_element_type=jnp.float32
    )
    projected = projected.astype(jnp.bfloat16)
    o_ref[:, :value_width] = projected[:, (HEADS + KVH) * HD :]
    row_patch = lax.broadcasted_iota(jnp.int32, (sub_rows, cols), 0) // BINS
    col_patch = lax.broadcasted_iota(jnp.int32, (sub_rows, cols), 1) // (group_size * BINS)
    same = row_patch == col_patch
    ones = jnp.ones((8, HD), jnp.bfloat16)
    for sg in range(rows_ref.shape[0] // sub_rows):
        base = sg * sub_rows
        xs = projected[base : base + sub_rows, :]
        for g in range(KVH):
            k = xs[:, (HEADS + g) * HD : (HEADS + g + 1) * HD]
            kf = k.astype(jnp.float32)
            k_scale = 1.0 / jnp.sqrt(jnp.mean(kf * kf, axis=-1, keepdims=True) + 1e-06)
            pieces = []
            for p in range(SUB):
                for r in range(group_size):
                    h = g * group_size + r
                    pieces.append(xs[p * BINS : (p + 1) * BINS, h * HD : (h + 1) * HD])
            q = jnp.concatenate(pieces, axis=0)
            qf = q.astype(jnp.float32)
            q2 = qf * qf
            q2_hi = q2.astype(jnp.bfloat16)
            q2_lo = (q2 - q2_hi.astype(jnp.float32)).astype(jnp.bfloat16)
            q_sums = lax.dot_general(
                ones, q2_hi, (((1,), (1,)), ((), ())), preferred_element_type=jnp.float32
            ) + lax.dot_general(
                ones, q2_lo, (((1,), (1,)), ((), ())), preferred_element_type=jnp.float32
            )
            q_sums = q_sums[0:1, :]
            q_scale = 1.0 / jnp.sqrt(q_sums / HD + 1e-06)
            raw = lax.dot_general(
                k, q, (((1,), (1,)), ((), ())), preferred_element_type=jnp.float32
            )
            s = raw * k_scale * q_scale / HD**0.5
            e = jnp.where(same, jnp.exp(s), 0.0)
            total = jnp.sum(e, axis=0, keepdims=True)
            w = (e * (1.0 / total)).astype(jnp.bfloat16).astype(jnp.float32)
            width = group_size * BINS
            for p in range(SUB):
                tile = w[p * BINS : (p + 1) * BINS, :]
                compact = tile[:, 0:width]
                for c in range(1, SUB):
                    compact = compact + tile[:, c * width : (c + 1) * width]
                row0 = base + p * BINS
                w_ref[row0 : row0 + BINS, g * width : (g + 1) * width] = compact
    o_ref[:, value_width:] = w_ref[...].astype(jnp.bfloat16)


def owner_payload(rows, merged_hi, merged_lo):
    total, depth = rows.shape
    width = merged_hi.shape[1]
    return pl.pallas_call(
        _owner_kernel,
        out_shape=jax.ShapeDtypeStruct((total, KVH * HD + HEADS * BINS), jnp.bfloat16),
        grid=(total // ROWS,),
        in_specs=[
            pl.BlockSpec((ROWS, depth), lambda i: (i, 0)),
            pl.BlockSpec((depth, width), lambda i: (0, 0)),
            pl.BlockSpec((depth, width), lambda i: (0, 0)),
        ],
        out_specs=pl.BlockSpec((ROWS, KVH * HD + HEADS * BINS), lambda i: (i, 0)),
        scratch_shapes=[pltpu.VMEM((ROWS, HEADS * BINS), jnp.float32)],
    )(rows, merged_hi, merged_lo)


def heads_from(payload):
    n = payload.shape[0]
    group_size = HEADS // KVH
    v = payload[:, :, : KVH * HD].reshape(n, BINS, KVH, HD)
    w = payload[:, :, KVH * HD :].reshape(n, BINS, KVH, group_size, BINS)
    mixed = jnp.einsum("pjgri,pjge->pigre", w, v, preferred_element_type=jnp.float32)
    return mixed.reshape(n, BINS, HEADS * HD).astype(jnp.bfloat16)


def body(power, bin_index, session, readin_weight, qkv_weight):
    wide_count = lax.axis_size("wide")
    seq_count = lax.axis_size("seq")
    wide_index = lax.axis_index("wide")
    seq_index = lax.axis_index("seq")
    sample_rows, channels = power.shape
    patch_count = channels // CH
    quarter = patch_count // seq_count
    bin_count = sample_rows // SPB
    all_bins = bin_count * seq_count

    signal = power.astype(jnp.float32)
    partial = jnp.sum(signal * signal, axis=0)
    received = [partial]
    for shift in range(1, seq_count):
        pairs = [(i, (i + shift) % seq_count) for i in range(seq_count)]
        received.append(lax.ppermute(partial, "seq", pairs))
    squares = received[0]
    for piece in received[1:]:
        squares = squares + piece
    inv_rms = 1.0 / jnp.sqrt(squares / (sample_rows * seq_count) + 1e-06)
    active = jnp.maximum(signal * inv_rms[None, :] - 0.8, 0.0)
    local_bins = bin_index - seq_index * bin_count
    sums = [
        jnp.sum(jnp.where((local_bins == b)[:, None], active, 0.0), axis=0) for b in range(bin_count)
    ]
    binned = (jnp.stack(sums) * (1.0 / SPB)).astype(jnp.bfloat16)
    binned = binned.reshape(bin_count, seq_count, quarter, CH).transpose(1, 0, 2, 3)
    received = [lax.dynamic_index_in_dim(binned, seq_index, 0, keepdims=False)]
    for shift in range(1, seq_count):
        pairs = [(i, (i + shift) % seq_count) for i in range(seq_count)]
        piece = lax.dynamic_index_in_dim(binned, (seq_index + shift) % seq_count, 0, keepdims=False)
        received.append(lax.ppermute(piece, "seq", pairs))
    order = (seq_index - jnp.arange(seq_count, dtype=jnp.int32)) % seq_count
    binned = jnp.take(jnp.stack(received), order, axis=0)
    block_rows = binned.reshape(all_bins, quarter, CH).transpose(1, 0, 2).reshape(
        quarter * all_bins, CH
    )

    block = wide_index * seq_count + seq_index
    owners = lax.dynamic_slice_in_dim(session, block * quarter, quarter)
    same = owners[:, None] == owners[None, :]
    earlier = jnp.arange(quarter)[None, :] < jnp.arange(quarter)[:, None]
    rank = jnp.sum((same & earlier).astype(jnp.int32), axis=1)
    slot = owners * CAP + rank
    slot_count = wide_count * CAP
    row_ids = jnp.arange(slot_count * all_bins, dtype=jnp.int32)
    col_ids = jnp.arange(quarter * all_bins, dtype=jnp.int32)
    col_slot = jnp.repeat(slot, all_bins)
    dispatch = (
        (row_ids[:, None] // all_bins == col_slot[None, :])
        & (row_ids[:, None] % all_bins == col_ids[None, :] % all_bins)
    ).astype(jnp.bfloat16)
    outgoing = jnp.dot(dispatch, block_rows, preferred_element_type=jnp.float32).astype(
        jnp.bfloat16
    )
    chunk = CAP * all_bins
    arrived = lax.all_to_all(
        outgoing.reshape(wide_count, chunk, CH), "wide", split_axis=0, concat_axis=0, tiled=True
    )
    weight_block = readin_weight[0]
    merged = jnp.dot(weight_block, qkv_weight, preferred_element_type=jnp.float32)
    merged_hi = merged.astype(jnp.bfloat16)
    merged_lo = (merged - merged_hi.astype(jnp.float32)).astype(jnp.bfloat16)
    rows = arrived.reshape(slot_count * all_bins, CH)
    payload = owner_payload(rows, merged_hi, merged_lo)
    returned = lax.all_to_all(
        payload.reshape(wide_count, chunk, -1), "wide", split_axis=0, concat_axis=0, tiled=True
    )
    returned = returned.reshape(slot_count * all_bins, -1)
    mine = jnp.dot(dispatch.T, returned, preferred_element_type=jnp.float32).astype(jnp.bfloat16)
    return heads_from(mine.reshape(quarter, all_bins, -1))


def solution(mesh):
    placed = (P("seq", "wide"), P("seq"), P(), P("wide", None, None), P())
    return jax.shard_map(
        body, mesh=mesh, in_specs=placed, out_specs=P(("wide", "seq"), None, None), check_vma=False
    )
```

```python
import jax
import jax.numpy as jnp
from jax import lax
from jax.experimental import pallas as pl
from jax.experimental.pallas import tpu as pltpu
from jax.sharding import PartitionSpec as P

CH = 128
HD = 128
HEADS = 8
KVH = 2
SPB = 20
CAP = 2
BINS = 8
ROWS = 256
SUB = 4


def _owner_kernel(rows_ref, hi_ref, lo_ref, o_ref, w_ref):
    group_size = HEADS // KVH
    sub_rows = SUB * BINS
    cols = SUB * group_size * BINS
    value_width = KVH * HD
    rows = rows_ref[...]
    projected = jnp.dot(rows, hi_ref[...], preferred_element_type=jnp.float32) + jnp.dot(
        rows, lo_ref[...], preferred_element_type=jnp.float32
    )
    projected = projected.astype(jnp.bfloat16)
    o_ref[:, :value_width] = projected[:, (HEADS + KVH) * HD :]
    row_patch = lax.broadcasted_iota(jnp.int32, (sub_rows, cols), 0) // BINS
    col_patch = lax.broadcasted_iota(jnp.int32, (sub_rows, cols), 1) // (group_size * BINS)
    same = row_patch == col_patch
    ones = jnp.ones((8, HD), jnp.bfloat16)
    for sg in range(rows_ref.shape[0] // sub_rows):
        base = sg * sub_rows
        xs = projected[base : base + sub_rows, :]
        for g in range(KVH):
            k = xs[:, (HEADS + g) * HD : (HEADS + g + 1) * HD]
            kf = k.astype(jnp.float32)
            k_scale = 1.0 / jnp.sqrt(jnp.mean(kf * kf, axis=-1, keepdims=True) + 1e-06)
            pieces = []
            for p in range(SUB):
                for r in range(group_size):
                    h = g * group_size + r
                    pieces.append(xs[p * BINS : (p + 1) * BINS, h * HD : (h + 1) * HD])
            q = jnp.concatenate(pieces, axis=0)
            qf = q.astype(jnp.float32)
            q2 = qf * qf
            q2_hi = q2.astype(jnp.bfloat16)
            q2_lo = (q2 - q2_hi.astype(jnp.float32)).astype(jnp.bfloat16)
            q_sums = lax.dot_general(
                ones, q2_hi, (((1,), (1,)), ((), ())), preferred_element_type=jnp.float32
            ) + lax.dot_general(
                ones, q2_lo, (((1,), (1,)), ((), ())), preferred_element_type=jnp.float32
            )
            q_sums = q_sums[0:1, :]
            q_scale = 1.0 / jnp.sqrt(q_sums / HD + 1e-06)
            raw = lax.dot_general(
                k, q, (((1,), (1,)), ((), ())), preferred_element_type=jnp.float32
            )
            s = raw * k_scale * q_scale / HD**0.5
            e = jnp.where(same, jnp.exp(s), 0.0)
            total = jnp.sum(e, axis=0, keepdims=True)
            w = (e * (1.0 / total)).astype(jnp.bfloat16).astype(jnp.float32)
            width = group_size * BINS
            for p in range(SUB):
                tile = w[p * BINS : (p + 1) * BINS, :]
                compact = tile[:, 0:width]
                for c in range(1, SUB):
                    compact = compact + tile[:, c * width : (c + 1) * width]
                row0 = base + p * BINS
                w_ref[row0 : row0 + BINS, g * width : (g + 1) * width] = compact
    o_ref[:, value_width:] = w_ref[...].astype(jnp.bfloat16)


def owner_payload(rows, merged_hi, merged_lo):
    total, depth = rows.shape
    width = merged_hi.shape[1]
    return pl.pallas_call(
        _owner_kernel,
        out_shape=jax.ShapeDtypeStruct((total, KVH * HD + HEADS * BINS), jnp.bfloat16),
        grid=(total // ROWS,),
        in_specs=[
            pl.BlockSpec((ROWS, depth), lambda i: (i, 0)),
            pl.BlockSpec((depth, width), lambda i: (0, 0)),
            pl.BlockSpec((depth, width), lambda i: (0, 0)),
        ],
        out_specs=pl.BlockSpec((ROWS, KVH * HD + HEADS * BINS), lambda i: (i, 0)),
        scratch_shapes=[pltpu.VMEM((ROWS, HEADS * BINS), jnp.float32)],
    )(rows, merged_hi, merged_lo)


def heads_from(payload):
    n = payload.shape[0]
    group_size = HEADS // KVH
    v = payload[:, :, : KVH * HD].reshape(n, BINS, KVH, HD)
    w = payload[:, :, KVH * HD :].reshape(n, BINS, KVH, group_size, BINS)
    mixed = jnp.einsum("pjgri,pjge->pigre", w, v, preferred_element_type=jnp.float32)
    return mixed.reshape(n, BINS, HEADS * HD).astype(jnp.bfloat16)


def body(power, bin_index, session, readin_weight, qkv_weight):
    wide_count = lax.axis_size("wide")
    seq_count = lax.axis_size("seq")
    wide_index = lax.axis_index("wide")
    seq_index = lax.axis_index("seq")
    sample_rows, channels = power.shape
    patch_count = channels // CH
    quarter = patch_count // seq_count
    bin_count = sample_rows // SPB
    all_bins = bin_count * seq_count

    signal = power.astype(jnp.float32)
    partial = jnp.sum(signal * signal, axis=0)
    received = [partial]
    for shift in range(1, seq_count):
        pairs = [(i, (i + shift) % seq_count) for i in range(seq_count)]
        received.append(lax.ppermute(partial, "seq", pairs))
    squares = received[0]
    for piece in received[1:]:
        squares = squares + piece
    inv_rms = 1.0 / jnp.sqrt(squares / (sample_rows * seq_count) + 1e-06)
    active = jnp.maximum(signal * inv_rms[None, :] - 0.8, 0.0)
    local_bins = bin_index - seq_index * bin_count
    sums = [
        jnp.sum(jnp.where((local_bins == b)[:, None], active, 0.0), axis=0) for b in range(bin_count)
    ]
    binned = (jnp.stack(sums) * (1.0 / SPB)).astype(jnp.bfloat16)
    binned = binned.reshape(bin_count, seq_count, quarter, CH).transpose(1, 0, 2, 3)
    received = [lax.dynamic_index_in_dim(binned, seq_index, 0, keepdims=False)]
    for shift in range(1, seq_count):
        pairs = [(i, (i + shift) % seq_count) for i in range(seq_count)]
        piece = lax.dynamic_index_in_dim(binned, (seq_index + shift) % seq_count, 0, keepdims=False)
        received.append(lax.ppermute(piece, "seq", pairs))
    order = (seq_index - jnp.arange(seq_count, dtype=jnp.int32)) % seq_count
    binned = jnp.take(jnp.stack(received), order, axis=0)
    block_rows = binned.reshape(all_bins, quarter, CH).transpose(1, 0, 2).reshape(
        quarter, all_bins * CH
    )

    block = wide_index * seq_count + seq_index
    owners = lax.dynamic_slice_in_dim(session, block * quarter, quarter)
    same = owners[:, None] == owners[None, :]
    earlier = jnp.arange(quarter)[None, :] < jnp.arange(quarter)[:, None]
    rank = jnp.sum((same & earlier).astype(jnp.int32), axis=1)
    slot = owners * CAP + rank
    slot_count = wide_count * CAP
    dispatch = (jnp.arange(slot_count, dtype=jnp.int32)[:, None] == slot[None, :]).astype(
        jnp.bfloat16
    )
    outgoing = jnp.dot(dispatch, block_rows, preferred_element_type=jnp.float32).astype(
        jnp.bfloat16
    )
    arrived = lax.all_to_all(outgoing, "wide", split_axis=0, concat_axis=0, tiled=True)
    weight_block = readin_weight[0]
    merged = jnp.dot(weight_block, qkv_weight, preferred_element_type=jnp.float32)
    merged_hi = merged.astype(jnp.bfloat16)
    merged_lo = (merged - merged_hi.astype(jnp.float32)).astype(jnp.bfloat16)
    rows = arrived.reshape(slot_count * all_bins, CH)
    payload = owner_payload(rows, merged_hi, merged_lo).reshape(slot_count, -1)
    returned = lax.all_to_all(payload, "wide", split_axis=0, concat_axis=0, tiled=True)
    mine = jnp.dot(dispatch.T, returned, preferred_element_type=jnp.float32).astype(jnp.bfloat16)
    return heads_from(mine.reshape(quarter, all_bins, -1))


def solution(mesh):
    placed = (P("seq", "wide"), P("seq"), P(), P("wide", None, None), P())
    return jax.shard_map(
        body, mesh=mesh, in_specs=placed, out_specs=P(("wide", "seq"), None, None), check_vma=False
    )
```

```python
import jax
import jax.numpy as jnp
from jax import lax
from jax.experimental import pallas as pl
from jax.experimental.pallas import tpu as pltpu
from jax.sharding import PartitionSpec as P

CH = 128
HD = 128
HEADS = 8
KVH = 2
SPB = 20
CAP = 2
BINS = 8
ROWS = 512
SUB = 4


def _owner_kernel(rows_ref, hi_ref, lo_ref, o_ref, w_ref):
    group_size = HEADS // KVH
    sub_rows = SUB * BINS
    cols = SUB * group_size * BINS
    value_width = KVH * HD
    rows = rows_ref[...]
    projected = jnp.dot(rows, hi_ref[...], preferred_element_type=jnp.float32) + jnp.dot(
        rows, lo_ref[...], preferred_element_type=jnp.float32
    )
    projected = projected.astype(jnp.bfloat16)
    o_ref[:, :value_width] = projected[:, (HEADS + KVH) * HD :]
    row_patch = lax.broadcasted_iota(jnp.int32, (sub_rows, cols), 0) // BINS
    col_patch = lax.broadcasted_iota(jnp.int32, (sub_rows, cols), 1) // (group_size * BINS)
    same = row_patch == col_patch
    ones = jnp.ones((8, HD), jnp.bfloat16)
    for sg in range(rows_ref.shape[0] // sub_rows):
        base = sg * sub_rows
        xs = projected[base : base + sub_rows, :]
        for g in range(KVH):
            k = xs[:, (HEADS + g) * HD : (HEADS + g + 1) * HD]
            kf = k.astype(jnp.float32)
            k_scale = 1.0 / jnp.sqrt(jnp.mean(kf * kf, axis=-1, keepdims=True) + 1e-06)
            pieces = []
            for p in range(SUB):
                for r in range(group_size):
                    h = g * group_size + r
                    pieces.append(xs[p * BINS : (p + 1) * BINS, h * HD : (h + 1) * HD])
            q = jnp.concatenate(pieces, axis=0)
            qf = q.astype(jnp.float32)
            q2 = qf * qf
            q2_hi = q2.astype(jnp.bfloat16)
            q2_lo = (q2 - q2_hi.astype(jnp.float32)).astype(jnp.bfloat16)
            q_sums = lax.dot_general(
                ones, q2_hi, (((1,), (1,)), ((), ())), preferred_element_type=jnp.float32
            ) + lax.dot_general(
                ones, q2_lo, (((1,), (1,)), ((), ())), preferred_element_type=jnp.float32
            )
            q_sums = q_sums[0:1, :]
            q_scale = 1.0 / jnp.sqrt(q_sums / HD + 1e-06)
            raw = lax.dot_general(
                k, q, (((1,), (1,)), ((), ())), preferred_element_type=jnp.float32
            )
            s = raw * k_scale * q_scale / HD**0.5
            e = jnp.where(same, jnp.exp(s), 0.0)
            total = jnp.sum(e, axis=0, keepdims=True)
            w = (e * (1.0 / total)).astype(jnp.bfloat16).astype(jnp.float32)
            width = group_size * BINS
            for p in range(SUB):
                tile = w[p * BINS : (p + 1) * BINS, :]
                compact = tile[:, 0:width]
                for c in range(1, SUB):
                    compact = compact + tile[:, c * width : (c + 1) * width]
                row0 = base + p * BINS
                w_ref[row0 : row0 + BINS, g * width : (g + 1) * width] = compact
    o_ref[:, value_width:] = w_ref[...].astype(jnp.bfloat16)


def owner_payload(rows, merged_hi, merged_lo):
    total, depth = rows.shape
    width = merged_hi.shape[1]
    return pl.pallas_call(
        _owner_kernel,
        out_shape=jax.ShapeDtypeStruct((total, KVH * HD + HEADS * BINS), jnp.bfloat16),
        grid=(total // ROWS,),
        in_specs=[
            pl.BlockSpec((ROWS, depth), lambda i: (i, 0)),
            pl.BlockSpec((depth, width), lambda i: (0, 0)),
            pl.BlockSpec((depth, width), lambda i: (0, 0)),
        ],
        out_specs=pl.BlockSpec((ROWS, KVH * HD + HEADS * BINS), lambda i: (i, 0)),
        scratch_shapes=[pltpu.VMEM((ROWS, HEADS * BINS), jnp.float32)],
    )(rows, merged_hi, merged_lo)


def heads_from(payload):
    n = payload.shape[0]
    group_size = HEADS // KVH
    v = payload[:, :, : KVH * HD].reshape(n, BINS, KVH, HD)
    w = payload[:, :, KVH * HD :].reshape(n, BINS, KVH, group_size, BINS)
    mixed = jnp.einsum("pjgri,pjge->pigre", w, v, preferred_element_type=jnp.float32)
    return mixed.reshape(n, BINS, HEADS * HD).astype(jnp.bfloat16)


def body(power, bin_index, session, readin_weight, qkv_weight):
    wide_count = lax.axis_size("wide")
    seq_count = lax.axis_size("seq")
    wide_index = lax.axis_index("wide")
    seq_index = lax.axis_index("seq")
    sample_rows, channels = power.shape
    patch_count = channels // CH
    quarter = patch_count // seq_count
    bin_count = sample_rows // SPB
    all_bins = bin_count * seq_count

    signal = power.astype(jnp.float32)
    partial = jnp.sum(signal * signal, axis=0)
    received = [partial]
    for shift in range(1, seq_count):
        pairs = [(i, (i + shift) % seq_count) for i in range(seq_count)]
        received.append(lax.ppermute(partial, "seq", pairs))
    squares = received[0]
    for piece in received[1:]:
        squares = squares + piece
    inv_rms = 1.0 / jnp.sqrt(squares / (sample_rows * seq_count) + 1e-06)
    active = jnp.maximum(signal * inv_rms[None, :] - 0.8, 0.0)
    local_bins = bin_index - seq_index * bin_count
    sums = [
        jnp.sum(jnp.where((local_bins == b)[:, None], active, 0.0), axis=0) for b in range(bin_count)
    ]
    binned = (jnp.stack(sums) * (1.0 / SPB)).astype(jnp.bfloat16)
    binned = binned.reshape(bin_count, seq_count, quarter, CH).transpose(1, 0, 2, 3)
    received = [lax.dynamic_index_in_dim(binned, seq_index, 0, keepdims=False)]
    for shift in range(1, seq_count):
        pairs = [(i, (i + shift) % seq_count) for i in range(seq_count)]
        piece = lax.dynamic_index_in_dim(binned, (seq_index + shift) % seq_count, 0, keepdims=False)
        received.append(lax.ppermute(piece, "seq", pairs))
    order = (seq_index - jnp.arange(seq_count, dtype=jnp.int32)) % seq_count
    binned = jnp.take(jnp.stack(received), order, axis=0)
    block_rows = binned.reshape(all_bins, quarter, CH).transpose(1, 0, 2).reshape(
        quarter, all_bins * CH
    )

    block = wide_index * seq_count + seq_index
    owners = lax.dynamic_slice_in_dim(session, block * quarter, quarter)
    same = owners[:, None] == owners[None, :]
    earlier = jnp.arange(quarter)[None, :] < jnp.arange(quarter)[:, None]
    rank = jnp.sum((same & earlier).astype(jnp.int32), axis=1)
    slot = owners * CAP + rank
    slot_count = wide_count * CAP
    dispatch = (jnp.arange(slot_count, dtype=jnp.int32)[:, None] == slot[None, :]).astype(
        jnp.bfloat16
    )
    outgoing = jnp.dot(dispatch, block_rows, preferred_element_type=jnp.float32).astype(
        jnp.bfloat16
    )
    arrived = lax.all_to_all(outgoing, "wide", split_axis=0, concat_axis=0, tiled=True)
    weight_block = readin_weight[0]
    merged = jnp.dot(weight_block, qkv_weight, preferred_element_type=jnp.float32)
    merged_hi = merged.astype(jnp.bfloat16)
    merged_lo = (merged - merged_hi.astype(jnp.float32)).astype(jnp.bfloat16)
    rows = arrived.reshape(slot_count * all_bins, CH)
    payload = owner_payload(rows, merged_hi, merged_lo).reshape(slot_count, -1)
    returned = lax.all_to_all(payload, "wide", split_axis=0, concat_axis=0, tiled=True)
    mine = jnp.dot(dispatch.T, returned, preferred_element_type=jnp.float32).astype(jnp.bfloat16)
    return heads_from(mine.reshape(quarter, all_bins, -1))


def solution(mesh):
    placed = (P("seq", "wide"), P("seq"), P(), P("wide", None, None), P())
    return jax.shard_map(
        body, mesh=mesh, in_specs=placed, out_specs=P(("wide", "seq"), None, None), check_vma=False
    )
```

```python
import jax
import jax.numpy as jnp
from jax import lax
from jax.experimental import pallas as pl
from jax.experimental.pallas import tpu as pltpu
from jax.sharding import PartitionSpec as P

CH = 128
HD = 128
HEADS = 8
KVH = 2
SPB = 20
CAP = 2
BINS = 8
ROWS = 1024
SUB = 4


def _owner_kernel(rows_ref, hi_ref, lo_ref, o_ref, w_ref):
    group_size = HEADS // KVH
    sub_rows = SUB * BINS
    cols = SUB * group_size * BINS
    value_width = KVH * HD
    rows = rows_ref[...]
    projected = jnp.dot(rows, hi_ref[...], preferred_element_type=jnp.float32) + jnp.dot(
        rows, lo_ref[...], preferred_element_type=jnp.float32
    )
    projected = projected.astype(jnp.bfloat16)
    o_ref[:, :value_width] = projected[:, (HEADS + KVH) * HD :]
    row_patch = lax.broadcasted_iota(jnp.int32, (sub_rows, cols), 0) // BINS
    col_patch = lax.broadcasted_iota(jnp.int32, (sub_rows, cols), 1) // (group_size * BINS)
    same = row_patch == col_patch
    ones = jnp.ones((8, HD), jnp.bfloat16)
    for sg in range(rows_ref.shape[0] // sub_rows):
        base = sg * sub_rows
        xs = projected[base : base + sub_rows, :]
        for g in range(KVH):
            k = xs[:, (HEADS + g) * HD : (HEADS + g + 1) * HD]
            kf = k.astype(jnp.float32)
            k_scale = 1.0 / jnp.sqrt(jnp.mean(kf * kf, axis=-1, keepdims=True) + 1e-06)
            pieces = []
            for p in range(SUB):
                for r in range(group_size):
                    h = g * group_size + r
                    pieces.append(xs[p * BINS : (p + 1) * BINS, h * HD : (h + 1) * HD])
            q = jnp.concatenate(pieces, axis=0)
            qf = q.astype(jnp.float32)
            q2 = qf * qf
            q2_hi = q2.astype(jnp.bfloat16)
            q2_lo = (q2 - q2_hi.astype(jnp.float32)).astype(jnp.bfloat16)
            q_sums = lax.dot_general(
                ones, q2_hi, (((1,), (1,)), ((), ())), preferred_element_type=jnp.float32
            ) + lax.dot_general(
                ones, q2_lo, (((1,), (1,)), ((), ())), preferred_element_type=jnp.float32
            )
            q_sums = q_sums[0:1, :]
            q_scale = 1.0 / jnp.sqrt(q_sums / HD + 1e-06)
            raw = lax.dot_general(
                k, q, (((1,), (1,)), ((), ())), preferred_element_type=jnp.float32
            )
            s = raw * k_scale * q_scale / HD**0.5
            e = jnp.where(same, jnp.exp(s), 0.0)
            total = jnp.sum(e, axis=0, keepdims=True)
            w = (e * (1.0 / total)).astype(jnp.bfloat16).astype(jnp.float32)
            width = group_size * BINS
            for p in range(SUB):
                tile = w[p * BINS : (p + 1) * BINS, :]
                compact = tile[:, 0:width]
                for c in range(1, SUB):
                    compact = compact + tile[:, c * width : (c + 1) * width]
                row0 = base + p * BINS
                w_ref[row0 : row0 + BINS, g * width : (g + 1) * width] = compact
    o_ref[:, value_width:] = w_ref[...].astype(jnp.bfloat16)


def owner_payload(rows, merged_hi, merged_lo):
    total, depth = rows.shape
    width = merged_hi.shape[1]
    return pl.pallas_call(
        _owner_kernel,
        out_shape=jax.ShapeDtypeStruct((total, KVH * HD + HEADS * BINS), jnp.bfloat16),
        grid=(total // ROWS,),
        in_specs=[
            pl.BlockSpec((ROWS, depth), lambda i: (i, 0)),
            pl.BlockSpec((depth, width), lambda i: (0, 0)),
            pl.BlockSpec((depth, width), lambda i: (0, 0)),
        ],
        out_specs=pl.BlockSpec((ROWS, KVH * HD + HEADS * BINS), lambda i: (i, 0)),
        scratch_shapes=[pltpu.VMEM((ROWS, HEADS * BINS), jnp.float32)],
    )(rows, merged_hi, merged_lo)


def heads_from(payload):
    n = payload.shape[0]
    group_size = HEADS // KVH
    v = payload[:, :, : KVH * HD].reshape(n, BINS, KVH, HD)
    w = payload[:, :, KVH * HD :].reshape(n, BINS, KVH, group_size, BINS)
    mixed = jnp.einsum("pjgri,pjge->pigre", w, v, preferred_element_type=jnp.float32)
    return mixed.reshape(n, BINS, HEADS * HD).astype(jnp.bfloat16)


def body(power, bin_index, session, readin_weight, qkv_weight):
    wide_count = lax.axis_size("wide")
    seq_count = lax.axis_size("seq")
    wide_index = lax.axis_index("wide")
    seq_index = lax.axis_index("seq")
    sample_rows, channels = power.shape
    patch_count = channels // CH
    quarter = patch_count // seq_count
    bin_count = sample_rows // SPB
    all_bins = bin_count * seq_count

    signal = power.astype(jnp.float32)
    partial = jnp.sum(signal * signal, axis=0)
    received = [partial]
    for shift in range(1, seq_count):
        pairs = [(i, (i + shift) % seq_count) for i in range(seq_count)]
        received.append(lax.ppermute(partial, "seq", pairs))
    squares = received[0]
    for piece in received[1:]:
        squares = squares + piece
    inv_rms = 1.0 / jnp.sqrt(squares / (sample_rows * seq_count) + 1e-06)
    active = jnp.maximum(signal * inv_rms[None, :] - 0.8, 0.0)
    local_bins = bin_index - seq_index * bin_count
    sums = [
        jnp.sum(jnp.where((local_bins == b)[:, None], active, 0.0), axis=0) for b in range(bin_count)
    ]
    binned = (jnp.stack(sums) * (1.0 / SPB)).astype(jnp.bfloat16)
    binned = binned.reshape(bin_count, seq_count, quarter, CH).transpose(1, 0, 2, 3)
    received = [lax.dynamic_index_in_dim(binned, seq_index, 0, keepdims=False)]
    for shift in range(1, seq_count):
        pairs = [(i, (i + shift) % seq_count) for i in range(seq_count)]
        piece = lax.dynamic_index_in_dim(binned, (seq_index + shift) % seq_count, 0, keepdims=False)
        received.append(lax.ppermute(piece, "seq", pairs))
    order = (seq_index - jnp.arange(seq_count, dtype=jnp.int32)) % seq_count
    binned = jnp.take(jnp.stack(received), order, axis=0)
    block_rows = binned.reshape(all_bins, quarter, CH).transpose(1, 0, 2).reshape(
        quarter, all_bins * CH
    )

    block = wide_index * seq_count + seq_index
    owners = lax.dynamic_slice_in_dim(session, block * quarter, quarter)
    same = owners[:, None] == owners[None, :]
    earlier = jnp.arange(quarter)[None, :] < jnp.arange(quarter)[:, None]
    rank = jnp.sum((same & earlier).astype(jnp.int32), axis=1)
    slot = owners * CAP + rank
    slot_count = wide_count * CAP
    dispatch = (jnp.arange(slot_count, dtype=jnp.int32)[:, None] == slot[None, :]).astype(
        jnp.bfloat16
    )
    outgoing = jnp.dot(dispatch, block_rows, preferred_element_type=jnp.float32).astype(
        jnp.bfloat16
    )
    arrived = lax.all_to_all(outgoing, "wide", split_axis=0, concat_axis=0, tiled=True)
    weight_block = readin_weight[0]
    merged = jnp.dot(weight_block, qkv_weight, preferred_element_type=jnp.float32)
    merged_hi = merged.astype(jnp.bfloat16)
    merged_lo = (merged - merged_hi.astype(jnp.float32)).astype(jnp.bfloat16)
    rows = arrived.reshape(slot_count * all_bins, CH)
    payload = owner_payload(rows, merged_hi, merged_lo).reshape(slot_count, -1)
    returned = lax.all_to_all(payload, "wide", split_axis=0, concat_axis=0, tiled=True)
    mine = jnp.dot(dispatch.T, returned, preferred_element_type=jnp.float32).astype(jnp.bfloat16)
    return heads_from(mine.reshape(quarter, all_bins, -1))


def solution(mesh):
    placed = (P("seq", "wide"), P("seq"), P(), P("wide", None, None), P())
    return jax.shard_map(
        body, mesh=mesh, in_specs=placed, out_specs=P(("wide", "seq"), None, None), check_vma=False
    )
```

```python
import jax
import jax.numpy as jnp
from jax import lax
from jax.experimental import pallas as pl
from jax.experimental.pallas import tpu as pltpu
from jax.sharding import PartitionSpec as P

CH = 128
HD = 128
HEADS = 8
KVH = 2
SPB = 20
CAP = 2
BINS = 8
ROWS = 512
SUB = 4


def _owner_kernel(rows_ref, hi_ref, lo_ref, o_ref, w_ref, v_ref):
    group_size = HEADS // KVH
    sub_rows = SUB * BINS
    cols = SUB * group_size * BINS
    value_width = KVH * HD
    rows = rows_ref[...]
    projected = jnp.dot(rows, hi_ref[...], preferred_element_type=jnp.float32) + jnp.dot(
        rows, lo_ref[...], preferred_element_type=jnp.float32
    )
    projected = projected.astype(jnp.bfloat16)
    for g in range(KVH):
        col = (HEADS + KVH + g) * HD
        v_ref[g] = projected[:, col : col + HD].astype(jnp.float32)
    row_patch = lax.broadcasted_iota(jnp.int32, (sub_rows, cols), 0) // BINS
    col_patch = lax.broadcasted_iota(jnp.int32, (sub_rows, cols), 1) // (group_size * BINS)
    same = row_patch == col_patch
    ones = jnp.ones((8, HD), jnp.bfloat16)
    for sg in range(rows_ref.shape[0] // sub_rows):
        base = sg * sub_rows
        xs = projected[base : base + sub_rows, :]
        for g in range(KVH):
            k = xs[:, (HEADS + g) * HD : (HEADS + g + 1) * HD]
            kf = k.astype(jnp.float32)
            k_scale = 1.0 / jnp.sqrt(jnp.mean(kf * kf, axis=-1, keepdims=True) + 1e-06)
            pieces = []
            for p in range(SUB):
                for r in range(group_size):
                    h = g * group_size + r
                    pieces.append(xs[p * BINS : (p + 1) * BINS, h * HD : (h + 1) * HD])
            q = jnp.concatenate(pieces, axis=0)
            qf = q.astype(jnp.float32)
            q2 = qf * qf
            q2_hi = q2.astype(jnp.bfloat16)
            q2_lo = (q2 - q2_hi.astype(jnp.float32)).astype(jnp.bfloat16)
            q_sums = lax.dot_general(
                ones, q2_hi, (((1,), (1,)), ((), ())), preferred_element_type=jnp.float32
            ) + lax.dot_general(
                ones, q2_lo, (((1,), (1,)), ((), ())), preferred_element_type=jnp.float32
            )
            q_sums = q_sums[0:1, :]
            q_scale = 1.0 / jnp.sqrt(q_sums / HD + 1e-06)
            raw = lax.dot_general(
                k, q, (((1,), (1,)), ((), ())), preferred_element_type=jnp.float32
            )
            s = raw * k_scale * q_scale / HD**0.5
            e = jnp.where(same, jnp.exp(s), 0.0)
            total = jnp.sum(e, axis=0, keepdims=True)
            w = (e * (1.0 / total)).astype(jnp.bfloat16).astype(jnp.float32)
            width = group_size * BINS
            for p in range(SUB):
                tile = w[p * BINS : (p + 1) * BINS, :]
                compact = tile[:, 0:width]
                for c in range(1, SUB):
                    compact = compact + tile[:, c * width : (c + 1) * width]
                row0 = base + p * BINS
                w_ref[row0 : row0 + BINS, g * width : (g + 1) * width] = compact
    slots = rows_ref.shape[0] // BINS
    weight_width = HEADS * BINS
    for j in range(BINS):
        picked = pl.ds(j, slots, stride=BINS)
        for g in range(KVH):
            col = j * value_width + g * HD
            o_ref[:, col : col + HD] = v_ref[g, picked, :].astype(jnp.bfloat16)
        base = BINS * value_width + j * weight_width
        o_ref[:, base : base + weight_width] = w_ref[picked, :][:, :weight_width].astype(jnp.bfloat16)


def owner_payload(rows, merged_hi, merged_lo):
    total, depth = rows.shape
    width = merged_hi.shape[1]
    return pl.pallas_call(
        _owner_kernel,
        out_shape=jax.ShapeDtypeStruct(
            (total // BINS, BINS * (KVH * HD + HEADS * BINS)), jnp.bfloat16
        ),
        grid=(total // ROWS,),
        in_specs=[
            pl.BlockSpec((ROWS, depth), lambda i: (i, 0)),
            pl.BlockSpec((depth, width), lambda i: (0, 0)),
            pl.BlockSpec((depth, width), lambda i: (0, 0)),
        ],
        out_specs=pl.BlockSpec(
            (ROWS // BINS, BINS * (KVH * HD + HEADS * BINS)), lambda i: (i, 0)
        ),
        scratch_shapes=[
            pltpu.VMEM((ROWS, HD), jnp.float32),
            pltpu.VMEM((KVH, ROWS, HD), jnp.float32),
        ],
    )(rows, merged_hi, merged_lo)


def heads_from(payload):
    n = payload.shape[0]
    group_size = HEADS // KVH
    split = BINS * KVH * HD
    v = payload[:, :split].reshape(n, BINS, KVH, HD)
    w = payload[:, split:].reshape(n, BINS, KVH, group_size, BINS)
    mixed = jnp.einsum("pjgri,pjge->pigre", w, v, preferred_element_type=jnp.float32)
    return mixed.reshape(n, BINS, HEADS * HD).astype(jnp.bfloat16)


def body(power, bin_index, session, readin_weight, qkv_weight):
    wide_count = lax.axis_size("wide")
    seq_count = lax.axis_size("seq")
    wide_index = lax.axis_index("wide")
    seq_index = lax.axis_index("seq")
    sample_rows, channels = power.shape
    patch_count = channels // CH
    quarter = patch_count // seq_count
    bin_count = sample_rows // SPB
    all_bins = bin_count * seq_count

    signal = power.astype(jnp.float32)
    partial = jnp.sum(signal * signal, axis=0)
    received = [partial]
    for shift in range(1, seq_count):
        pairs = [(i, (i + shift) % seq_count) for i in range(seq_count)]
        received.append(lax.ppermute(partial, "seq", pairs))
    squares = received[0]
    for piece in received[1:]:
        squares = squares + piece
    inv_rms = 1.0 / jnp.sqrt(squares / (sample_rows * seq_count) + 1e-06)
    active = jnp.maximum(signal * inv_rms[None, :] - 0.8, 0.0)
    local_bins = bin_index - seq_index * bin_count
    sums = [
        jnp.sum(jnp.where((local_bins == b)[:, None], active, 0.0), axis=0) for b in range(bin_count)
    ]
    binned = (jnp.stack(sums) * (1.0 / SPB)).astype(jnp.bfloat16)
    binned = binned.reshape(bin_count, seq_count, quarter, CH).transpose(1, 0, 2, 3)
    received = [lax.dynamic_index_in_dim(binned, seq_index, 0, keepdims=False)]
    for shift in range(1, seq_count):
        pairs = [(i, (i + shift) % seq_count) for i in range(seq_count)]
        piece = lax.dynamic_index_in_dim(binned, (seq_index + shift) % seq_count, 0, keepdims=False)
        received.append(lax.ppermute(piece, "seq", pairs))
    order = (seq_index - jnp.arange(seq_count, dtype=jnp.int32)) % seq_count
    binned = jnp.take(jnp.stack(received), order, axis=0)
    block_rows = binned.reshape(all_bins, quarter, CH).transpose(1, 0, 2).reshape(
        quarter, all_bins * CH
    )

    block = wide_index * seq_count + seq_index
    owners = lax.dynamic_slice_in_dim(session, block * quarter, quarter)
    same = owners[:, None] == owners[None, :]
    earlier = jnp.arange(quarter)[None, :] < jnp.arange(quarter)[:, None]
    rank = jnp.sum((same & earlier).astype(jnp.int32), axis=1)
    slot = owners * CAP + rank
    slot_count = wide_count * CAP
    dispatch = (jnp.arange(slot_count, dtype=jnp.int32)[:, None] == slot[None, :]).astype(
        jnp.bfloat16
    )
    outgoing = jnp.dot(dispatch, block_rows, preferred_element_type=jnp.float32).astype(
        jnp.bfloat16
    )
    arrived = lax.all_to_all(outgoing, "wide", split_axis=0, concat_axis=0, tiled=True)
    weight_block = readin_weight[0]
    merged = jnp.dot(weight_block, qkv_weight, preferred_element_type=jnp.float32)
    merged_hi = merged.astype(jnp.bfloat16)
    merged_lo = (merged - merged_hi.astype(jnp.float32)).astype(jnp.bfloat16)
    rows = arrived.reshape(slot_count * all_bins, CH)
    payload = owner_payload(rows, merged_hi, merged_lo).reshape(slot_count, -1)
    returned = lax.all_to_all(payload, "wide", split_axis=0, concat_axis=0, tiled=True)
    mine = jnp.dot(dispatch.T, returned, preferred_element_type=jnp.float32).astype(jnp.bfloat16)
    return heads_from(mine)


def solution(mesh):
    placed = (P("seq", "wide"), P("seq"), P(), P("wide", None, None), P())
    return jax.shard_map(
        body, mesh=mesh, in_specs=placed, out_specs=P(("wide", "seq"), None, None), check_vma=False
    )
```

```python
import jax
import jax.numpy as jnp
from jax import lax
from jax.experimental import pallas as pl
from jax.experimental.pallas import tpu as pltpu
from jax.sharding import PartitionSpec as P

CH = 128
HD = 128
HEADS = 8
KVH = 2
SPB = 20
CAP = 2
BINS = 8
ROWS = 512
SUB = 8


def _owner_kernel(rows_ref, hi_ref, lo_ref, o_ref, w_ref):
    group_size = HEADS // KVH
    sub_rows = SUB * BINS
    cols = SUB * group_size * BINS
    value_width = KVH * HD
    rows = rows_ref[...]
    projected = jnp.dot(rows, hi_ref[...], preferred_element_type=jnp.float32) + jnp.dot(
        rows, lo_ref[...], preferred_element_type=jnp.float32
    )
    projected = projected.astype(jnp.bfloat16)
    o_ref[:, :value_width] = projected[:, (HEADS + KVH) * HD :]
    row_patch = lax.broadcasted_iota(jnp.int32, (sub_rows, cols), 0) // BINS
    col_patch = lax.broadcasted_iota(jnp.int32, (sub_rows, cols), 1) // (group_size * BINS)
    same = row_patch == col_patch
    ones = jnp.ones((8, HD), jnp.bfloat16)
    for sg in range(rows_ref.shape[0] // sub_rows):
        base = sg * sub_rows
        xs = projected[base : base + sub_rows, :]
        for g in range(KVH):
            k = xs[:, (HEADS + g) * HD : (HEADS + g + 1) * HD]
            kf = k.astype(jnp.float32)
            k_scale = 1.0 / jnp.sqrt(jnp.mean(kf * kf, axis=-1, keepdims=True) + 1e-06)
            pieces = []
            for p in range(SUB):
                for r in range(group_size):
                    h = g * group_size + r
                    pieces.append(xs[p * BINS : (p + 1) * BINS, h * HD : (h + 1) * HD])
            q = jnp.concatenate(pieces, axis=0)
            qf = q.astype(jnp.float32)
            q2 = qf * qf
            q2_hi = q2.astype(jnp.bfloat16)
            q2_lo = (q2 - q2_hi.astype(jnp.float32)).astype(jnp.bfloat16)
            q_sums = lax.dot_general(
                ones, q2_hi, (((1,), (1,)), ((), ())), preferred_element_type=jnp.float32
            ) + lax.dot_general(
                ones, q2_lo, (((1,), (1,)), ((), ())), preferred_element_type=jnp.float32
            )
            q_sums = q_sums[0:1, :]
            q_scale = 1.0 / jnp.sqrt(q_sums / HD + 1e-06)
            raw = lax.dot_general(
                k, q, (((1,), (1,)), ((), ())), preferred_element_type=jnp.float32
            )
            s = raw * k_scale * q_scale / HD**0.5
            e = jnp.where(same, jnp.exp(s), 0.0)
            total = jnp.sum(e, axis=0, keepdims=True)
            w = (e * (1.0 / total)).astype(jnp.bfloat16).astype(jnp.float32)
            width = group_size * BINS
            for p in range(SUB):
                tile = w[p * BINS : (p + 1) * BINS, :]
                compact = tile[:, 0:width]
                for c in range(1, SUB):
                    compact = compact + tile[:, c * width : (c + 1) * width]
                row0 = base + p * BINS
                w_ref[row0 : row0 + BINS, g * width : (g + 1) * width] = compact
    o_ref[:, value_width:] = w_ref[...].astype(jnp.bfloat16)


def owner_payload(rows, merged_hi, merged_lo):
    total, depth = rows.shape
    width = merged_hi.shape[1]
    return pl.pallas_call(
        _owner_kernel,
        out_shape=jax.ShapeDtypeStruct((total, KVH * HD + HEADS * BINS), jnp.bfloat16),
        grid=(total // ROWS,),
        in_specs=[
            pl.BlockSpec((ROWS, depth), lambda i: (i, 0)),
            pl.BlockSpec((depth, width), lambda i: (0, 0)),
            pl.BlockSpec((depth, width), lambda i: (0, 0)),
        ],
        out_specs=pl.BlockSpec((ROWS, KVH * HD + HEADS * BINS), lambda i: (i, 0)),
        scratch_shapes=[pltpu.VMEM((ROWS, HEADS * BINS), jnp.float32)],
    )(rows, merged_hi, merged_lo)


def heads_from(payload):
    n = payload.shape[0]
    group_size = HEADS // KVH
    v = payload[:, :, : KVH * HD].reshape(n, BINS, KVH, HD)
    w = payload[:, :, KVH * HD :].reshape(n, BINS, KVH, group_size, BINS)
    mixed = jnp.einsum("pjgri,pjge->pigre", w, v, preferred_element_type=jnp.float32)
    return mixed.reshape(n, BINS, HEADS * HD).astype(jnp.bfloat16)


def body(power, bin_index, session, readin_weight, qkv_weight):
    wide_count = lax.axis_size("wide")
    seq_count = lax.axis_size("seq")
    wide_index = lax.axis_index("wide")
    seq_index = lax.axis_index("seq")
    sample_rows, channels = power.shape
    patch_count = channels // CH
    quarter = patch_count // seq_count
    bin_count = sample_rows // SPB
    all_bins = bin_count * seq_count

    signal = power.astype(jnp.float32)
    partial = jnp.sum(signal * signal, axis=0)
    received = [partial]
    for shift in range(1, seq_count):
        pairs = [(i, (i + shift) % seq_count) for i in range(seq_count)]
        received.append(lax.ppermute(partial, "seq", pairs))
    squares = received[0]
    for piece in received[1:]:
        squares = squares + piece
    inv_rms = 1.0 / jnp.sqrt(squares / (sample_rows * seq_count) + 1e-06)
    active = jnp.maximum(signal * inv_rms[None, :] - 0.8, 0.0)
    local_bins = bin_index - seq_index * bin_count
    sums = [
        jnp.sum(jnp.where((local_bins == b)[:, None], active, 0.0), axis=0) for b in range(bin_count)
    ]
    binned = (jnp.stack(sums) * (1.0 / SPB)).astype(jnp.bfloat16)
    binned = binned.reshape(bin_count, seq_count, quarter, CH).transpose(1, 0, 2, 3)
    received = [lax.dynamic_index_in_dim(binned, seq_index, 0, keepdims=False)]
    for shift in range(1, seq_count):
        pairs = [(i, (i + shift) % seq_count) for i in range(seq_count)]
        piece = lax.dynamic_index_in_dim(binned, (seq_index + shift) % seq_count, 0, keepdims=False)
        received.append(lax.ppermute(piece, "seq", pairs))
    order = (seq_index - jnp.arange(seq_count, dtype=jnp.int32)) % seq_count
    binned = jnp.take(jnp.stack(received), order, axis=0)
    block_rows = binned.reshape(all_bins, quarter, CH).transpose(1, 0, 2).reshape(
        quarter, all_bins * CH
    )

    block = wide_index * seq_count + seq_index
    owners = lax.dynamic_slice_in_dim(session, block * quarter, quarter)
    same = owners[:, None] == owners[None, :]
    earlier = jnp.arange(quarter)[None, :] < jnp.arange(quarter)[:, None]
    rank = jnp.sum((same & earlier).astype(jnp.int32), axis=1)
    slot = owners * CAP + rank
    slot_count = wide_count * CAP
    dispatch = (jnp.arange(slot_count, dtype=jnp.int32)[:, None] == slot[None, :]).astype(
        jnp.bfloat16
    )
    outgoing = jnp.dot(dispatch, block_rows, preferred_element_type=jnp.float32).astype(
        jnp.bfloat16
    )
    arrived = lax.all_to_all(outgoing, "wide", split_axis=0, concat_axis=0, tiled=True)
    weight_block = readin_weight[0]
    merged = jnp.dot(weight_block, qkv_weight, preferred_element_type=jnp.float32)
    merged_hi = merged.astype(jnp.bfloat16)
    merged_lo = (merged - merged_hi.astype(jnp.float32)).astype(jnp.bfloat16)
    rows = arrived.reshape(slot_count * all_bins, CH)
    payload = owner_payload(rows, merged_hi, merged_lo).reshape(slot_count, -1)
    returned = lax.all_to_all(payload, "wide", split_axis=0, concat_axis=0, tiled=True)
    mine = jnp.dot(dispatch.T, returned, preferred_element_type=jnp.float32).astype(jnp.bfloat16)
    return heads_from(mine.reshape(quarter, all_bins, -1))


def solution(mesh):
    placed = (P("seq", "wide"), P("seq"), P(), P("wide", None, None), P())
    return jax.shard_map(
        body, mesh=mesh, in_specs=placed, out_specs=P(("wide", "seq"), None, None), check_vma=False
    )
```

```python
import jax
import jax.numpy as jnp
from jax import lax
from jax.experimental import pallas as pl
from jax.experimental.pallas import tpu as pltpu
from jax.sharding import PartitionSpec as P

CH = 128
HD = 128
HEADS = 8
KVH = 2
SPB = 20
CAP = 2
BINS = 8
ROWS = 512
SUB = 16


def _owner_kernel(rows_ref, hi_ref, lo_ref, o_ref, w_ref):
    group_size = HEADS // KVH
    sub_rows = SUB * BINS
    cols = SUB * group_size * BINS
    value_width = KVH * HD
    rows = rows_ref[...]
    projected = jnp.dot(rows, hi_ref[...], preferred_element_type=jnp.float32) + jnp.dot(
        rows, lo_ref[...], preferred_element_type=jnp.float32
    )
    projected = projected.astype(jnp.bfloat16)
    o_ref[:, :value_width] = projected[:, (HEADS + KVH) * HD :]
    row_patch = lax.broadcasted_iota(jnp.int32, (sub_rows, cols), 0) // BINS
    col_patch = lax.broadcasted_iota(jnp.int32, (sub_rows, cols), 1) // (group_size * BINS)
    same = row_patch == col_patch
    ones = jnp.ones((8, HD), jnp.bfloat16)
    for sg in range(rows_ref.shape[0] // sub_rows):
        base = sg * sub_rows
        xs = projected[base : base + sub_rows, :]
        for g in range(KVH):
            k = xs[:, (HEADS + g) * HD : (HEADS + g + 1) * HD]
            kf = k.astype(jnp.float32)
            k_scale = 1.0 / jnp.sqrt(jnp.mean(kf * kf, axis=-1, keepdims=True) + 1e-06)
            pieces = []
            for p in range(SUB):
                for r in range(group_size):
                    h = g * group_size + r
                    pieces.append(xs[p * BINS : (p + 1) * BINS, h * HD : (h + 1) * HD])
            q = jnp.concatenate(pieces, axis=0)
            qf = q.astype(jnp.float32)
            q2 = qf * qf
            q2_hi = q2.astype(jnp.bfloat16)
            q2_lo = (q2 - q2_hi.astype(jnp.float32)).astype(jnp.bfloat16)
            q_sums = lax.dot_general(
                ones, q2_hi, (((1,), (1,)), ((), ())), preferred_element_type=jnp.float32
            ) + lax.dot_general(
                ones, q2_lo, (((1,), (1,)), ((), ())), preferred_element_type=jnp.float32
            )
            q_sums = q_sums[0:1, :]
            q_scale = 1.0 / jnp.sqrt(q_sums / HD + 1e-06)
            raw = lax.dot_general(
                k, q, (((1,), (1,)), ((), ())), preferred_element_type=jnp.float32
            )
            s = raw * k_scale * q_scale / HD**0.5
            e = jnp.where(same, jnp.exp(s), 0.0)
            total = jnp.sum(e, axis=0, keepdims=True)
            w = (e * (1.0 / total)).astype(jnp.bfloat16).astype(jnp.float32)
            width = group_size * BINS
            for p in range(SUB):
                tile = w[p * BINS : (p + 1) * BINS, :]
                compact = tile[:, 0:width]
                for c in range(1, SUB):
                    compact = compact + tile[:, c * width : (c + 1) * width]
                row0 = base + p * BINS
                w_ref[row0 : row0 + BINS, g * width : (g + 1) * width] = compact
    o_ref[:, value_width:] = w_ref[...].astype(jnp.bfloat16)


def owner_payload(rows, merged_hi, merged_lo):
    total, depth = rows.shape
    width = merged_hi.shape[1]
    return pl.pallas_call(
        _owner_kernel,
        out_shape=jax.ShapeDtypeStruct((total, KVH * HD + HEADS * BINS), jnp.bfloat16),
        grid=(total // ROWS,),
        in_specs=[
            pl.BlockSpec((ROWS, depth), lambda i: (i, 0)),
            pl.BlockSpec((depth, width), lambda i: (0, 0)),
            pl.BlockSpec((depth, width), lambda i: (0, 0)),
        ],
        out_specs=pl.BlockSpec((ROWS, KVH * HD + HEADS * BINS), lambda i: (i, 0)),
        scratch_shapes=[pltpu.VMEM((ROWS, HEADS * BINS), jnp.float32)],
    )(rows, merged_hi, merged_lo)


def heads_from(payload):
    n = payload.shape[0]
    group_size = HEADS // KVH
    v = payload[:, :, : KVH * HD].reshape(n, BINS, KVH, HD)
    w = payload[:, :, KVH * HD :].reshape(n, BINS, KVH, group_size, BINS)
    mixed = jnp.einsum("pjgri,pjge->pigre", w, v, preferred_element_type=jnp.float32)
    return mixed.reshape(n, BINS, HEADS * HD).astype(jnp.bfloat16)


def body(power, bin_index, session, readin_weight, qkv_weight):
    wide_count = lax.axis_size("wide")
    seq_count = lax.axis_size("seq")
    wide_index = lax.axis_index("wide")
    seq_index = lax.axis_index("seq")
    sample_rows, channels = power.shape
    patch_count = channels // CH
    quarter = patch_count // seq_count
    bin_count = sample_rows // SPB
    all_bins = bin_count * seq_count

    signal = power.astype(jnp.float32)
    partial = jnp.sum(signal * signal, axis=0)
    received = [partial]
    for shift in range(1, seq_count):
        pairs = [(i, (i + shift) % seq_count) for i in range(seq_count)]
        received.append(lax.ppermute(partial, "seq", pairs))
    squares = received[0]
    for piece in received[1:]:
        squares = squares + piece
    inv_rms = 1.0 / jnp.sqrt(squares / (sample_rows * seq_count) + 1e-06)
    active = jnp.maximum(signal * inv_rms[None, :] - 0.8, 0.0)
    local_bins = bin_index - seq_index * bin_count
    sums = [
        jnp.sum(jnp.where((local_bins == b)[:, None], active, 0.0), axis=0) for b in range(bin_count)
    ]
    binned = (jnp.stack(sums) * (1.0 / SPB)).astype(jnp.bfloat16)
    binned = binned.reshape(bin_count, seq_count, quarter, CH).transpose(1, 0, 2, 3)
    received = [lax.dynamic_index_in_dim(binned, seq_index, 0, keepdims=False)]
    for shift in range(1, seq_count):
        pairs = [(i, (i + shift) % seq_count) for i in range(seq_count)]
        piece = lax.dynamic_index_in_dim(binned, (seq_index + shift) % seq_count, 0, keepdims=False)
        received.append(lax.ppermute(piece, "seq", pairs))
    order = (seq_index - jnp.arange(seq_count, dtype=jnp.int32)) % seq_count
    binned = jnp.take(jnp.stack(received), order, axis=0)
    block_rows = binned.reshape(all_bins, quarter, CH).transpose(1, 0, 2).reshape(
        quarter, all_bins * CH
    )

    block = wide_index * seq_count + seq_index
    owners = lax.dynamic_slice_in_dim(session, block * quarter, quarter)
    same = owners[:, None] == owners[None, :]
    earlier = jnp.arange(quarter)[None, :] < jnp.arange(quarter)[:, None]
    rank = jnp.sum((same & earlier).astype(jnp.int32), axis=1)
    slot = owners * CAP + rank
    slot_count = wide_count * CAP
    dispatch = (jnp.arange(slot_count, dtype=jnp.int32)[:, None] == slot[None, :]).astype(
        jnp.bfloat16
    )
    outgoing = jnp.dot(dispatch, block_rows, preferred_element_type=jnp.float32).astype(
        jnp.bfloat16
    )
    arrived = lax.all_to_all(outgoing, "wide", split_axis=0, concat_axis=0, tiled=True)
    weight_block = readin_weight[0]
    merged = jnp.dot(weight_block, qkv_weight, preferred_element_type=jnp.float32)
    merged_hi = merged.astype(jnp.bfloat16)
    merged_lo = (merged - merged_hi.astype(jnp.float32)).astype(jnp.bfloat16)
    rows = arrived.reshape(slot_count * all_bins, CH)
    payload = owner_payload(rows, merged_hi, merged_lo).reshape(slot_count, -1)
    returned = lax.all_to_all(payload, "wide", split_axis=0, concat_axis=0, tiled=True)
    mine = jnp.dot(dispatch.T, returned, preferred_element_type=jnp.float32).astype(jnp.bfloat16)
    return heads_from(mine.reshape(quarter, all_bins, -1))


def solution(mesh):
    placed = (P("seq", "wide"), P("seq"), P(), P("wide", None, None), P())
    return jax.shard_map(
        body, mesh=mesh, in_specs=placed, out_specs=P(("wide", "seq"), None, None), check_vma=False
    )
```

```python
import jax
import jax.numpy as jnp
from jax import lax
from jax.experimental import pallas as pl
from jax.experimental.pallas import tpu as pltpu
from jax.sharding import PartitionSpec as P

CH = 128
HD = 128
HEADS = 8
KVH = 2
SPB = 20
CAP = 2
BINS = 8
ROWS = 512
SUB = 8


def _owner_kernel(rows_ref, hi_ref, lo_ref, o_ref, w_ref):
    group_size = HEADS // KVH
    sub_rows = SUB * BINS
    cols = SUB * group_size * BINS
    value_width = KVH * HD
    rows = rows_ref[...]
    projected = jnp.dot(rows, hi_ref[...], preferred_element_type=jnp.float32) + jnp.dot(
        rows, lo_ref[...], preferred_element_type=jnp.float32
    )
    projected = projected.astype(jnp.bfloat16)
    o_ref[:, :value_width] = projected[:, (HEADS + KVH) * HD :]
    row_patch = lax.broadcasted_iota(jnp.int32, (sub_rows, cols), 0) // BINS
    col_patch = lax.broadcasted_iota(jnp.int32, (sub_rows, cols), 1) // (group_size * BINS)
    same = row_patch == col_patch
    ones = jnp.ones((8, HD), jnp.bfloat16)
    for sg in range(rows_ref.shape[0] // sub_rows):
        base = sg * sub_rows
        xs = projected[base : base + sub_rows, :]
        for g in range(KVH):
            k = xs[:, (HEADS + g) * HD : (HEADS + g + 1) * HD]
            kf = k.astype(jnp.float32)
            k_scale = 1.0 / jnp.sqrt(jnp.mean(kf * kf, axis=-1, keepdims=True) + 1e-06)
            pieces = []
            for p in range(SUB):
                for r in range(group_size):
                    h = g * group_size + r
                    pieces.append(xs[p * BINS : (p + 1) * BINS, h * HD : (h + 1) * HD])
            q = jnp.concatenate(pieces, axis=0)
            qf = q.astype(jnp.float32)
            q2 = qf * qf
            q2_hi = q2.astype(jnp.bfloat16)
            q2_lo = (q2 - q2_hi.astype(jnp.float32)).astype(jnp.bfloat16)
            q_sums = lax.dot_general(
                ones, q2_hi, (((1,), (1,)), ((), ())), preferred_element_type=jnp.float32
            ) + lax.dot_general(
                ones, q2_lo, (((1,), (1,)), ((), ())), preferred_element_type=jnp.float32
            )
            q_sums = q_sums[0:1, :]
            q_scale = 1.0 / jnp.sqrt(q_sums / HD + 1e-06)
            raw = lax.dot_general(
                k, q, (((1,), (1,)), ((), ())), preferred_element_type=jnp.float32
            )
            s = raw * k_scale * q_scale / HD**0.5
            e = jnp.where(same, jnp.exp(s), 0.0)
            total = jnp.sum(e, axis=0, keepdims=True)
            w = (e * (1.0 / total)).astype(jnp.bfloat16).astype(jnp.float32)
            width = group_size * BINS
            for p in range(SUB):
                tile = w[p * BINS : (p + 1) * BINS, :]
                compact = tile[:, 0:width]
                for c in range(1, SUB):
                    compact = compact + tile[:, c * width : (c + 1) * width]
                row0 = base + p * BINS
                w_ref[row0 : row0 + BINS, g * width : (g + 1) * width] = compact
    o_ref[:, value_width:] = w_ref[...].astype(jnp.bfloat16)


def owner_payload(rows, merged_hi, merged_lo):
    total, depth = rows.shape
    width = merged_hi.shape[1]
    return pl.pallas_call(
        _owner_kernel,
        out_shape=jax.ShapeDtypeStruct((total, KVH * HD + HEADS * BINS), jnp.bfloat16),
        grid=(total // ROWS,),
        in_specs=[
            pl.BlockSpec((ROWS, depth), lambda i: (i, 0)),
            pl.BlockSpec((depth, width), lambda i: (0, 0)),
            pl.BlockSpec((depth, width), lambda i: (0, 0)),
        ],
        out_specs=pl.BlockSpec((ROWS, KVH * HD + HEADS * BINS), lambda i: (i, 0)),
        scratch_shapes=[pltpu.VMEM((ROWS, HEADS * BINS), jnp.float32)],
    )(rows, merged_hi, merged_lo)


def heads_from(payload):
    n = payload.shape[0]
    group_size = HEADS // KVH
    v = payload[:, :, : KVH * HD].reshape(n, BINS, KVH, HD)
    w = payload[:, :, KVH * HD :].reshape(n, BINS, KVH, group_size, BINS)
    mixed = jnp.einsum("pjgri,pjge->pigre", w, v, preferred_element_type=jnp.float32)
    return mixed.reshape(n, BINS, HEADS * HD).astype(jnp.bfloat16)


def body(power, bin_index, session, readin_weight, qkv_weight):
    wide_count = lax.axis_size("wide")
    seq_count = lax.axis_size("seq")
    wide_index = lax.axis_index("wide")
    seq_index = lax.axis_index("seq")
    sample_rows, channels = power.shape
    patch_count = channels // CH
    quarter = patch_count // seq_count
    bin_count = sample_rows // SPB
    all_bins = bin_count * seq_count

    signal = power.astype(jnp.float32)
    partial = jnp.sum(signal * signal, axis=0)
    received = [partial]
    for shift in range(1, seq_count):
        pairs = [(i, (i + shift) % seq_count) for i in range(seq_count)]
        received.append(lax.ppermute(partial, "seq", pairs))
    squares = received[0]
    for piece in received[1:]:
        squares = squares + piece
    inv_rms = 1.0 / jnp.sqrt(squares / (sample_rows * seq_count) + 1e-06)
    active = jnp.maximum(signal * inv_rms[None, :] - 0.8, 0.0)
    local_bins = bin_index - seq_index * bin_count
    sums = [
        jnp.sum(jnp.where((local_bins == b)[:, None], active, 0.0), axis=0) for b in range(bin_count)
    ]
    binned = (jnp.stack(sums) * (1.0 / SPB)).astype(jnp.bfloat16)
    binned = binned.reshape(bin_count, seq_count, quarter, CH).transpose(1, 0, 2, 3)
    received = [lax.dynamic_index_in_dim(binned, seq_index, 0, keepdims=False)]
    for shift in range(1, seq_count):
        pairs = [(i, (i + shift) % seq_count) for i in range(seq_count)]
        piece = lax.dynamic_index_in_dim(binned, (seq_index + shift) % seq_count, 0, keepdims=False)
        received.append(lax.ppermute(piece, "seq", pairs))
    flipped = jnp.stack(received[::-1])
    doubled = jnp.concatenate([flipped, flipped], axis=0)
    start = (seq_count - 1 - seq_index) % seq_count
    binned = lax.dynamic_slice_in_dim(doubled, start, seq_count, axis=0)
    block_rows = binned.reshape(all_bins, quarter, CH).transpose(1, 0, 2).reshape(
        quarter, all_bins * CH
    )

    block = wide_index * seq_count + seq_index
    owners = lax.dynamic_slice_in_dim(session, block * quarter, quarter)
    same = owners[:, None] == owners[None, :]
    earlier = jnp.arange(quarter)[None, :] < jnp.arange(quarter)[:, None]
    rank = jnp.sum((same & earlier).astype(jnp.int32), axis=1)
    slot = owners * CAP + rank
    slot_count = wide_count * CAP
    dispatch = (jnp.arange(slot_count, dtype=jnp.int32)[:, None] == slot[None, :]).astype(
        jnp.bfloat16
    )
    outgoing = jnp.dot(dispatch, block_rows, preferred_element_type=jnp.float32).astype(
        jnp.bfloat16
    )
    arrived = lax.all_to_all(outgoing, "wide", split_axis=0, concat_axis=0, tiled=True)
    weight_block = readin_weight[0]
    merged = jnp.dot(weight_block, qkv_weight, preferred_element_type=jnp.float32)
    merged_hi = merged.astype(jnp.bfloat16)
    merged_lo = (merged - merged_hi.astype(jnp.float32)).astype(jnp.bfloat16)
    rows = arrived.reshape(slot_count * all_bins, CH)
    payload = owner_payload(rows, merged_hi, merged_lo).reshape(slot_count, -1)
    returned = lax.all_to_all(payload, "wide", split_axis=0, concat_axis=0, tiled=True)
    mine = jnp.dot(dispatch.T, returned, preferred_element_type=jnp.float32).astype(jnp.bfloat16)
    return heads_from(mine.reshape(quarter, all_bins, -1))


def solution(mesh):
    placed = (P("seq", "wide"), P("seq"), P(), P("wide", None, None), P())
    return jax.shard_map(
        body, mesh=mesh, in_specs=placed, out_specs=P(("wide", "seq"), None, None), check_vma=False
    )
```
